256 devices in a mesh: tile: 128 (over z, x, y), chan: 2 (over core).
Axes of the slice: x: 4, y: 4, z: 8, core: 2. Of those that a mesh axis runs over, the one named last changes fastest.
Arguments:
- jacobian: bfloat16 [1024, 616, 411], P('tile', 'chan'), may hold values from -0.3125 to 0.3125
- r_inverse: bfloat16 [616, 616], P('chan'), as said below
- innovation: bfloat16 [1024, 616], P('tile', 'chan'), may hold values from -6 to 6
- increments: bfloat16 [2048, 128, 411], P('tile'), may hold values from -6 to 6
- owner_offset: int32 [1024, 1], P('tile'), may hold values from 0 to 3; in each aligned block of 8 rows (0 to 7, 8 to 15, ...) at most 3 rows name the same one
- column_slot: int32 [1024], P('tile'), may hold values from 0 to 15
- foot_counts: int32 [128], P('tile'), may hold values from 1 to 8, as said below
Outputs:
- gradient: bfloat16 [2048, 128, 411], P('tile')
The draws below stay inside these ranges and needn't reach their ends.
Inputs may be any that keep to these rules, and one draw needn't show every extreme that they name: r_inverse is symmetric. `owner_offset`: the 8 footprints of one tile name each value at most 3 times, and some tile names some value exactly 3 times. `foot_counts`: each count is 8 divided by 1, 2, 4 or 8; some tile has 8.
All inputs are finite; a program needn't handle non-finite values.
Results may differ from the reference program's by a relative error of at most 0.0052.
Values may be sent and summed in bfloat16 or wider, within the bound.
No kernel may reach another device: no remote copies, remote signals or barrier semaphores. Data moves between devices by JAX's collectives and lax.ppermute only.
A program may use at most 64 MiB of HBM per device.

```python
import math
import jax
import jax.numpy as jnp
import numpy as np
from jax import lax

CH = 616
STATE = 411
MEMBERS = 128
F_DEV = 8
COL_DEV = 16
SPAN = 4
CAP = 3
FOOT = 1024
COLUMNS = 2048
N_TILE = 128


def draw_r_inverse(key, part):
    first, second = jax.random.split(jax.random.fold_in(key, 11))
    spread = 0.3 / math.sqrt(2.0 * CH)
    base = jax.random.normal(first, (CH, CH), jnp.float32) * spread
    diagonal = jax.random.uniform(second, (CH,), jnp.float32, 1.0, 2.0)
    paired = base + base.T
    index = jnp.arange(CH)
    on_diag = index[:, None] == index[None, :]
    full = jnp.where(on_diag, diagonal[:, None] + jnp.zeros_like(paired), paired)
    return full.astype(jnp.bfloat16)


def draw_foot_counts(key, part):
    first, second = jax.random.split(jax.random.fold_in(key, 23))
    shifts = jax.random.randint(first, (N_TILE,), 0, 4)
    divisors = jnp.array([1, 2, 4, 8], jnp.int32)
    counts = F_DEV // jnp.take(divisors, shifts)
    fullest = jax.random.randint(second, (), 0, N_TILE)
    counts = jnp.where(jnp.arange(N_TILE) == fullest, F_DEV, counts)
    return counts.astype(jnp.int32)


def touch_ends(result, own_key, low, high):
    dims = result.shape
    place = [jax.random.randint(jax.random.fold_in(own_key, axis), (), 0, dims[axis]) for axis in range(len(dims))]
    result = result.at[tuple(place)].set(low)
    longest = dims.index(max(dims))
    place[longest] = (place[longest] + 1) % dims[longest]
    return result.at[tuple(place)].set(high)


def steps_of(rng, shape, cuts, least, largest):
    def one(dim, blocks):
        draws = jax.random.uniform(jax.random.fold_in(jax.random.fold_in(rng, 6), dim), (blocks,), jnp.float32, least / len(cuts), largest / len(cuts))
        return jnp.repeat(jnp.exp(draws), shape[dim] // blocks).reshape((-1,) + (1,) * (len(shape) - dim - 1))

    gain = one(*cuts[0])
    for cut in cuts[1:]:
        gain = gain * one(*cut)
    return gain


def routed_block(key, own, number, rows, count, top, bound, skew):
    order = jax.random.permutation(key, count)
    heavy_load, usual = portions_of(count, rows * top, bound, skew, True), portions_of(count, rows * top, bound, skew, False)
    places = jnp.arange(count)

    def named(sizes, turn):
        used = int((sizes > 0).sum())
        fixed = max(1, used // 4)
        shifted = fixed + (places - fixed + turn * (used - fixed)) % max(1, count - fixed)
        return jnp.zeros((count,), jnp.int32).at[order[jnp.where(places < fixed, places, shifted)]].set(jnp.asarray(sizes, jnp.int32))

    sizes = jnp.where(number % 4 == 0, named(heavy_load, number // 4), named(usual, number - number // 4 - 1))
    mixed = jax.random.permutation(jax.random.fold_in(own, 3), count)
    source_of, taker = mixed[0:count // 2 * 2:2], mixed[1:count // 2 * 2:2]
    margin = jnp.minimum(sizes[source_of] - 1, bound - sizes[taker]) // 2
    margin = jnp.where((source_of == order[0]) | (taker == order[0]) | (sizes[taker] == 0), 0, jnp.maximum(margin, 0))
    shifted = jax.random.randint(jax.random.fold_in(own, 4), (count // 2,), 0, 1 << 20) % (margin + 1)
    sizes = sizes.at[source_of].add(-shifted).at[taker].add(shifted)
    members = jnp.searchsorted(jnp.cumsum(sizes), jnp.arange(rows * top), side="right").astype(jnp.int32)
    table = members.reshape(top, rows).T
    table = table[jax.random.permutation(jax.random.fold_in(own, 1), rows)]
    turn = jax.random.randint(jax.random.fold_in(own, 2), (rows, 1), 0, top)
    return jnp.take_along_axis(table, (jnp.arange(top)[None, :] + turn) % top, axis=1)


def portions_of(count, total, bound, skew, full):
    loads = [(1 << 20) // math.isqrt(standing ** skew) + 1 for standing in range(1, count + 1)]
    largest = bound if full else min(bound, max(-(-total // count), total * loads[0] // sum(loads)))
    least = 1 if total - largest >= count - 1 else 0
    holding, rest = [largest] + [least] * (count - 1), total - largest - least * (count - 1)
    while rest > 0:
        movable = [i for i in range(1, count) if holding[i] < largest] or [i for i in range(1, count) if holding[i] < bound]
        whole, remaining = sum([loads[i] for i in movable]), rest
        for i in movable:
            addition = min(bound - holding[i], max(1, remaining * loads[i] // whole), rest)
            holding[i] = holding[i] + addition
            rest = rest - addition
    return np.array(holding)


def noise(stream_key, extent, scale, reach, cuts=(), held_as=jnp.bfloat16):
    factor_of = steps_of(stream_key, extent, cuts, -0.22, 0.18) if cuts else 1.0
    values = jax.random.normal(stream_key, extent, jnp.float32) * scale * factor_of
    return jnp.minimum(jnp.maximum(values, -reach), reach).astype(held_as)


def setup_inputs(seed: int = 0) -> dict:
    keys = jax.random.split(jax.random.key(seed), 8)
    jacobian = noise(keys[0], (FOOT, CH, STATE), STATE ** -0.5, 0.3125, ((0, 128), (1, 2)))
    r_inverse = draw_r_inverse(jax.random.fold_in(keys[7], 71), 0)
    innovation = noise(keys[2], (FOOT, CH), 1.0, 6.0, ((0, 128), (1, 2)))
    increments = noise(keys[3], (COLUMNS, MEMBERS, STATE), 1.0, 6.0, ((0, 128),))
    owner_offset_keys = jax.random.split(jax.random.fold_in(keys[4], 1), FOOT // F_DEV)
    owner_offset_turns = jax.random.permutation(jax.random.fold_in(keys[4], 3), FOOT // F_DEV)
    owner_offset = jax.vmap(lambda own, number: routed_block(jax.random.fold_in(keys[4], 2), own, number, F_DEV, SPAN, 1, CAP, 2))(owner_offset_keys, owner_offset_turns).reshape((FOOT, 1))
    column_slot = touch_ends(jax.random.randint(keys[5], (FOOT,), 0, COL_DEV), jax.random.fold_in(keys[5], 1), 0, COL_DEV - 1).astype(jnp.int32)
    foot_counts = draw_foot_counts(jax.random.fold_in(keys[7], 71), 0)
    return {"jacobian": jacobian, "r_inverse": r_inverse, "innovation": innovation, "increments": increments, "owner_offset": owner_offset, "column_slot": column_slot, "foot_counts": foot_counts}


def reference(jacobian, r_inverse, innovation, increments, owner_offset, column_slot, foot_counts):
    order = jnp.arange(FOOT, dtype=jnp.int32)
    tile_of = order // F_DEV
    owner = (tile_of + owner_offset[:, 0] - 1) % N_TILE
    column = (owner * COL_DEV + column_slot).astype(jnp.int32)
    valid = (order % F_DEV) < jnp.take(foot_counts, tile_of)
    r_full = r_inverse.astype(jnp.float32)

    def per_tile(items):
        jac_tile, innov_tile, col_tile, valid_tile = items
        jac32 = jac_tile.astype(jnp.float32)
        states = jnp.take(increments, col_tile, axis=0).astype(jnp.float32)
        evolved = jnp.einsum('fks,fms->fmk', jac32, states)
        departure = (evolved - innov_tile.astype(jnp.float32)[:, None, :]).astype(jnp.bfloat16)
        weighted = jnp.einsum('ik,fmk->fmi', r_full, departure.astype(jnp.float32)).astype(jnp.bfloat16)
        adjoint = jnp.einsum('fks,fmk->fms', jac32, weighted.astype(jnp.float32))
        adjoint = jnp.where(valid_tile[:, None, None], adjoint, jnp.zeros_like(adjoint))
        return adjoint.astype(jnp.bfloat16)

    adjoint_all = lax.map(per_tile, (
        jacobian.reshape(N_TILE, F_DEV, CH, STATE),
        innovation.reshape(N_TILE, F_DEV, CH),
        column.reshape(N_TILE, F_DEV),
        valid.reshape(N_TILE, F_DEV)))
    adjoint_all = adjoint_all.reshape(FOOT, MEMBERS, STATE)
    total = jnp.zeros((COLUMNS, MEMBERS, STATE), jnp.float32)
    total = total.at[column].add(adjoint_all.astype(jnp.float32))
    return total.astype(jnp.bfloat16)
```

```python
import jax
import jax.numpy as jnp
from jax import lax
from jax.sharding import PartitionSpec as P

SPAN = 4
CAP = 3


def passed_along(value, axis, by):
    count = lax.axis_size(axis)
    return lax.ppermute(value, axis, [(i, (i + by) % count) for i in range(count)])


def passed_across(value, by):
    tiles = lax.axis_size("tile")
    cores = lax.axis_size("chan")
    pairs = []
    for t in range(tiles):
        for c in range(cores):
            pairs.append((t * cores + c, ((t + by) % tiles) * cores + (cores - 1 - c)))
    return lax.ppermute(value, ("tile", "chan"), pairs)


def swapped(value):
    return lax.ppermute(value, "chan", [(0, 1), (1, 0)])


def one_hot_rows(index, size):
    return (index[:, None] == jnp.arange(size, dtype=jnp.int32)[None, :]).astype(jnp.bfloat16)


def on_device(jacobian, r_inverse, innovation, increments, owner_offset, column_slot, foot_counts):
    foot = jacobian.shape[0]
    half_ch = jacobian.shape[1]
    state = jacobian.shape[2]
    columns = increments.shape[0]
    members = increments.shape[1]
    cores = lax.axis_size("chan")
    half_m = members // cores
    core = lax.axis_index("chan")
    capacity = CAP
    slots_total = SPAN * capacity

    jac_full = jnp.concatenate([jacobian, swapped(jacobian)], axis=1)
    innov_full = jnp.concatenate([innovation, swapped(innovation)], axis=1).astype(jnp.float32)
    r_rows = jnp.concatenate([r_inverse, swapped(r_inverse)], axis=0)
    r_full = jnp.roll(r_rows, -core * half_ch, axis=1)

    offset = owner_offset[:, 0]
    order = jnp.arange(foot, dtype=jnp.int32)
    earlier = (offset[:, None] == offset[None, :]) & (order[None, :] < order[:, None])
    rank = jnp.sum(earlier.astype(jnp.int32), axis=1)
    place = offset * capacity + rank
    select = (place[None, :] == jnp.arange(slots_total, dtype=jnp.int32)[:, None]).astype(jnp.bfloat16)
    request = jnp.sum(jnp.where(select > 0, column_slot[None, :], 0), axis=1)

    own_inc = lax.dynamic_slice_in_dim(increments, core * half_m, half_m, axis=1)
    own_inc = own_inc.reshape(columns, half_m * state)

    def pick(index):
        return jnp.dot(one_hot_rows(index, columns), own_inc,
                       preferred_element_type=jnp.float32).astype(jnp.bfloat16)

    fetched_parts = []
    slot_parts = []
    for g in range(SPAN):
        wanted = request[g * capacity:(g + 1) * capacity]
        if g == 1:
            fetched_parts.append(pick(wanted))
            slot_parts.append(wanted)
        else:
            asked = passed_along(wanted, "tile", g - 1)
            fetched_parts.append(passed_along(pick(asked), "tile", 1 - g))
            slot_parts.append(asked)
    fetched = jnp.concatenate(fetched_parts, axis=0)
    column_state = jnp.dot(select.T, fetched, preferred_element_type=jnp.float32).astype(jnp.bfloat16)
    column_state = column_state.reshape(foot, half_m, state)

    evolved = jnp.einsum("fks,fms->fmk", jac_full, column_state, preferred_element_type=jnp.float32)
    departure = (evolved - innov_full[:, None, :]).astype(jnp.bfloat16)
    weighted = jnp.einsum("fmk,ik->fmi", departure, r_full,
                          preferred_element_type=jnp.float32).astype(jnp.bfloat16)
    adjoint = jnp.einsum("fks,fmk->fms", jac_full, weighted, preferred_element_type=jnp.float32)
    live = jnp.arange(foot, dtype=jnp.int32) < foot_counts[0]
    adjoint = jnp.where(live[:, None, None], adjoint, 0.0).astype(jnp.bfloat16)

    packed = jnp.dot(select, adjoint.reshape(foot, half_m * state),
                     preferred_element_type=jnp.float32).astype(jnp.bfloat16)
    same_parts = []
    other_parts = []
    for g in range(SPAN):
        piece = packed[g * capacity:(g + 1) * capacity]
        if g == 1:
            same_parts.append(piece)
            other_parts.append(swapped(piece))
        else:
            same_parts.append(passed_along(piece, "tile", g - 1))
            other_parts.append(passed_across(piece, g - 1))
    got_slots = jnp.concatenate(slot_parts, axis=0)
    assign = one_hot_rows(got_slots, columns).T
    grad_same = jnp.dot(assign, jnp.concatenate(same_parts, axis=0),
                        preferred_element_type=jnp.float32).astype(jnp.bfloat16)
    grad_other = jnp.dot(assign, jnp.concatenate(other_parts, axis=0),
                         preferred_element_type=jnp.float32).astype(jnp.bfloat16)
    low = jnp.where(core == 0, grad_same, grad_other).reshape(columns, half_m, state)
    high = jnp.where(core == 0, grad_other, grad_same).reshape(columns, half_m, state)
    return jnp.concatenate([low, high], axis=1)


def solution(mesh):
    in_specs = (
        P("tile", "chan", None),
        P("chan", None),
        P("tile", "chan"),
        P("tile", None, None),
        P("tile", None),
        P("tile"),
        P("tile"),
    )
    out_specs = P("tile", None, None)
    return jax.shard_map(
        on_device, mesh=mesh, in_specs=in_specs, out_specs=out_specs, check_vma=False
    )
```

```python
import jax
import jax.numpy as jnp
from jax import lax
from jax.experimental import pallas as pl
from jax.experimental.pallas import tpu as pltpu
from jax.sharding import PartitionSpec as P

SPAN = 4
CAP = 3

NT = (((1,), (1,)), ((), ()))


def passed_along(value, axis, by):
    count = lax.axis_size(axis)
    return lax.ppermute(value, axis, [(i, (i + by) % count) for i in range(count)])


def swapped(value):
    return lax.ppermute(value, "chan", [(0, 1), (1, 0)])


def one_hot(index, size):
    return (index[:, None] == jnp.arange(size, dtype=jnp.int32)[None, :]).astype(jnp.bfloat16)


def adjoint_kernel(place_ref, count_ref, state_ref, jc_ref, jo_ref, ic_ref, io_ref,
                   rcc_ref, rco_ref, roc_ref, roo_ref, out_ref):
    f = pl.program_id(0)
    s = state_ref[0]
    jc = jc_ref[0]
    jo = jo_ref[0]
    ev_c = lax.dot_general(s, jc, NT, preferred_element_type=jnp.float32)
    ev_o = lax.dot_general(s, jo, NT, preferred_element_type=jnp.float32)
    dep_c = (ev_c - ic_ref[pl.ds(f, 1), :]).astype(jnp.bfloat16)
    dep_o = (ev_o - io_ref[pl.ds(f, 1), :]).astype(jnp.bfloat16)
    w_c = (jnp.dot(dep_c, rcc_ref[...], preferred_element_type=jnp.float32)
           + jnp.dot(dep_o, roc_ref[...], preferred_element_type=jnp.float32)).astype(jnp.bfloat16)
    w_o = (jnp.dot(dep_c, rco_ref[...], preferred_element_type=jnp.float32)
           + jnp.dot(dep_o, roo_ref[...], preferred_element_type=jnp.float32)).astype(jnp.bfloat16)
    adj = (jnp.dot(w_c, jc, preferred_element_type=jnp.float32)
           + jnp.dot(w_o, jo, preferred_element_type=jnp.float32))
    live = f < count_ref[0]
    out_ref[0] = jnp.where(live, adj, 0.0).astype(out_ref.dtype)


def adjoints(place, count, fetched, jac_c, jac_o, innov_c, innov_o, r_blocks):
    foot, half_ch, state = jac_c.shape
    half_m = fetched.shape[1]
    full = lambda f, p, n: (0, 0)
    grid_spec = pltpu.PrefetchScalarGridSpec(
        num_scalar_prefetch=2,
        grid=(foot,),
        in_specs=[
            pl.BlockSpec((1, half_m, state), lambda f, p, n: (p[f], 0, 0)),
            pl.BlockSpec((1, half_ch, state), lambda f, p, n: (f, 0, 0)),
            pl.BlockSpec((1, half_ch, state), lambda f, p, n: (f, 0, 0)),
            pl.BlockSpec((foot, half_ch), full),
            pl.BlockSpec((foot, half_ch), full),
        ] + [pl.BlockSpec((half_ch, half_ch), full) for _ in range(4)],
        out_specs=pl.BlockSpec((1, half_m, state), lambda f, p, n: (f, 0, 0)),
    )
    return pl.pallas_call(
        adjoint_kernel,
        grid_spec=grid_spec,
        out_shape=jax.ShapeDtypeStruct((foot, half_m, state), jnp.bfloat16),
    )(place, count, fetched, jac_c, jac_o, innov_c, innov_o, *r_blocks)


def on_device(jacobian, r_inverse, innovation, increments, owner_offset, column_slot, foot_counts):
    foot = jacobian.shape[0]
    half_ch = jacobian.shape[1]
    columns = increments.shape[0]
    members = increments.shape[1]
    cores = lax.axis_size("chan")
    half_m = members // cores
    core = lax.axis_index("chan")
    capacity = CAP
    slots_total = SPAN * capacity

    jac_o = swapped(jacobian)
    innov_c = innovation.astype(jnp.float32)
    innov_o = swapped(innovation).astype(jnp.float32)
    r_o = swapped(r_inverse)
    own_cols = core * half_ch
    other_cols = (1 - core) * half_ch
    r_blocks = (
        lax.dynamic_slice_in_dim(r_inverse, own_cols, half_ch, axis=1),
        lax.dynamic_slice_in_dim(r_inverse, other_cols, half_ch, axis=1),
        lax.dynamic_slice_in_dim(r_o, own_cols, half_ch, axis=1),
        lax.dynamic_slice_in_dim(r_o, other_cols, half_ch, axis=1),
    )

    offset = owner_offset[:, 0]
    order = jnp.arange(foot, dtype=jnp.int32)
    earlier = (offset[:, None] == offset[None, :]) & (order[None, :] < order[:, None])
    rank = jnp.sum(earlier.astype(jnp.int32), axis=1)
    place = offset * capacity + rank
    hit = place[None, :] == jnp.arange(slots_total, dtype=jnp.int32)[:, None]
    request = jnp.sum(jnp.where(hit, column_slot[None, :], 0), axis=1)

    own_inc = lax.dynamic_slice_in_dim(increments, core * half_m, half_m, axis=1)

    def pick(index):
        return jnp.einsum("ac,cms->ams", one_hot(index, columns), own_inc,
                          preferred_element_type=jnp.float32).astype(jnp.bfloat16)

    fetched_parts = []
    slot_parts = []
    for g in range(SPAN):
        wanted = request[g * capacity:(g + 1) * capacity]
        if g == 1:
            fetched_parts.append(pick(wanted))
            slot_parts.append(wanted)
        else:
            asked = passed_along(wanted, "tile", g - 1)
            fetched_parts.append(passed_along(pick(asked), "tile", 1 - g))
            slot_parts.append(asked)
    fetched = jnp.concatenate(fetched_parts, axis=0)

    adjoint = adjoints(place, foot_counts, fetched, jacobian, jac_o, innov_c, innov_o, r_blocks)

    packed = jnp.einsum("af,fmd->amd", hit.astype(jnp.bfloat16), adjoint,
                        preferred_element_type=jnp.float32).astype(jnp.bfloat16)
    recv_parts = []
    for g in range(SPAN):
        piece = packed[g * capacity:(g + 1) * capacity]
        if g == 1:
            recv_parts.append(piece)
        else:
            recv_parts.append(passed_along(piece, "tile", g - 1))
    got_slots = jnp.concatenate(slot_parts, axis=0)
    mine = jnp.einsum("ac,amd->cmd", one_hot(got_slots, columns), jnp.concatenate(recv_parts, axis=0),
                      preferred_element_type=jnp.float32).astype(jnp.bfloat16)
    other = swapped(mine)
    return jnp.where(core == 0, jnp.concatenate([mine, other], axis=1),
                     jnp.concatenate([other, mine], axis=1))


def solution(mesh):
    in_specs = (
        P("tile", "chan", None),
        P("chan", None),
        P("tile", "chan"),
        P("tile", None, None),
        P("tile", None),
        P("tile"),
        P("tile"),
    )
    out_specs = P("tile", None, None)
    return jax.shard_map(
        on_device, mesh=mesh, in_specs=in_specs, out_specs=out_specs, check_vma=False
    )
```

```python
import jax
import jax.numpy as jnp
from jax import lax
from jax.experimental import pallas as pl
from jax.experimental.pallas import tpu as pltpu
from jax.sharding import PartitionSpec as P

SPAN = 4
CAP = 3

NT = (((1,), (1,)), ((), ()))


def passed_along(value, axis, by):
    count = lax.axis_size(axis)
    return lax.ppermute(value, axis, [(i, (i + by) % count) for i in range(count)])


def swapped(value):
    return lax.ppermute(value, "chan", [(0, 1), (1, 0)])


def one_hot(index, size):
    return (index[:, None] == jnp.arange(size, dtype=jnp.int32)[None, :]).astype(jnp.bfloat16)


def adjoint_kernel(place_ref, count_ref, s0_ref, s1_ref, s2_ref, s3_ref, jc_ref, jo_ref, ic_ref, io_ref,
                   rcc_ref, rco_ref, roc_ref, roo_ref, out_ref):
    f = pl.program_id(0)
    group = place_ref[f] // CAP
    s = jnp.where(group == 0, s0_ref[0], jnp.where(group == 1, s1_ref[0],
                  jnp.where(group == 2, s2_ref[0], s3_ref[0])))
    jc = jc_ref[0]
    jo = jo_ref[0]
    ev_c = lax.dot_general(s, jc, NT, preferred_element_type=jnp.float32)
    ev_o = lax.dot_general(s, jo, NT, preferred_element_type=jnp.float32)
    dep_c = (ev_c - ic_ref[pl.ds(f, 1), :]).astype(jnp.bfloat16)
    dep_o = (ev_o - io_ref[pl.ds(f, 1), :]).astype(jnp.bfloat16)
    w_c = (jnp.dot(dep_c, rcc_ref[...], preferred_element_type=jnp.float32)
           + jnp.dot(dep_o, roc_ref[...], preferred_element_type=jnp.float32)).astype(jnp.bfloat16)
    w_o = (jnp.dot(dep_c, rco_ref[...], preferred_element_type=jnp.float32)
           + jnp.dot(dep_o, roo_ref[...], preferred_element_type=jnp.float32)).astype(jnp.bfloat16)
    adj = (jnp.dot(w_c, jc, preferred_element_type=jnp.float32)
           + jnp.dot(w_o, jo, preferred_element_type=jnp.float32))
    live = f < count_ref[0]
    out_ref[0] = jnp.where(live, adj, 0.0).astype(out_ref.dtype)


def copy_kernel(x_ref, o_ref):
    o_ref[...] = x_ref[...]


def row_major(x):
    block = (1,) + x.shape[1:]
    spec = pl.BlockSpec(block, lambda i: (i,) + (0,) * (x.ndim - 1))
    return pl.pallas_call(copy_kernel, grid=(x.shape[0],), in_specs=[spec], out_specs=spec,
                          out_shape=jax.ShapeDtypeStruct(x.shape, x.dtype))(x)


def adjoints(place, count, fetched, jac_c, jac_o, innov_c, innov_o, r_blocks):
    foot, half_ch, state = jac_c.shape
    half_m = fetched[0].shape[1]
    full = lambda f, p, n: (0, 0)

    def part(g):
        return pl.BlockSpec((1, half_m, state),
                            lambda f, p, n: (jnp.where(p[f] // CAP == g, p[f] % CAP, 0), 0, 0))

    grid_spec = pltpu.PrefetchScalarGridSpec(
        num_scalar_prefetch=2,
        grid=(foot,),
        in_specs=[
            part(0), part(1), part(2), part(3),
            pl.BlockSpec((1, half_ch, state), lambda f, p, n: (f, 0, 0)),
            pl.BlockSpec((1, half_ch, state), lambda f, p, n: (f, 0, 0)),
            pl.BlockSpec((foot, half_ch), full),
            pl.BlockSpec((foot, half_ch), full),
        ] + [pl.BlockSpec((half_ch, half_ch), full) for _ in range(4)],
        out_specs=pl.BlockSpec((1, half_m, state), lambda f, p, n: (f, 0, 0)),
    )
    return pl.pallas_call(
        adjoint_kernel,
        grid_spec=grid_spec,
        out_shape=jax.ShapeDtypeStruct((foot, half_m, state), jnp.bfloat16),
    )(place, count, *fetched, jac_c, jac_o, innov_c, innov_o, *r_blocks)


def on_device(jacobian, r_inverse, innovation, increments, owner_offset, column_slot, foot_counts):
    foot = jacobian.shape[0]
    half_ch = jacobian.shape[1]
    columns = increments.shape[0]
    members = increments.shape[1]
    cores = lax.axis_size("chan")
    half_m = members // cores
    core = lax.axis_index("chan")
    capacity = CAP
    slots_total = SPAN * capacity

    jac_c = jacobian
    jac_o = row_major(swapped(jacobian))
    innov_c = innovation.astype(jnp.float32)
    innov_o = swapped(innovation).astype(jnp.float32)
    r_o = swapped(r_inverse)
    first = core == 0
    rows_lo = jnp.where(first, r_inverse, r_o)
    rows_hi = jnp.where(first, r_o, r_inverse)
    r00, r01 = rows_lo[:, :half_ch], rows_lo[:, half_ch:]
    r10, r11 = rows_hi[:, :half_ch], rows_hi[:, half_ch:]
    r_blocks = (
        jnp.where(first, r00, r11),
        jnp.where(first, r01, r10),
        jnp.where(first, r10, r01),
        jnp.where(first, r11, r00),
    )

    offset = owner_offset[:, 0]
    order = jnp.arange(foot, dtype=jnp.int32)
    earlier = (offset[:, None] == offset[None, :]) & (order[None, :] < order[:, None])
    rank = jnp.sum(earlier.astype(jnp.int32), axis=1)
    place = offset * capacity + rank
    hit = place[None, :] == jnp.arange(slots_total, dtype=jnp.int32)[:, None]
    request = jnp.sum(jnp.where(hit, column_slot[None, :], 0), axis=1)

    own_inc = lax.dynamic_slice_in_dim(increments, core * half_m, half_m, axis=1)

    def pick(index):
        return jnp.einsum("ac,cms->ams", one_hot(index, columns), own_inc,
                          preferred_element_type=jnp.float32).astype(jnp.bfloat16)

    slot_parts = []
    for g in range(SPAN):
        wanted = request[g * capacity:(g + 1) * capacity]
        slot_parts.append(wanted if g == 1 else passed_along(wanted, "tile", g - 1))
    slot_parts, jac_o, r_blocks = lax.optimization_barrier((slot_parts, jac_o, r_blocks))
    fetched_parts = []
    for g in range(SPAN):
        picked = pick(slot_parts[g])
        fetched_parts.append(picked if g == 1 else passed_along(picked, "tile", 1 - g))
    adjoint = adjoints(place, foot_counts, fetched_parts, jac_c, jac_o, innov_c, innov_o, r_blocks)

    packed = jnp.einsum("af,fmd->amd", hit.astype(jnp.bfloat16), adjoint,
                        preferred_element_type=jnp.float32).astype(jnp.bfloat16)
    recv_parts = []
    for g in range(SPAN):
        piece = packed[g * capacity:(g + 1) * capacity]
        if g == 1:
            recv_parts.append(piece)
        else:
            recv_parts.append(passed_along(piece, "tile", g - 1))
    got_slots = jnp.concatenate(slot_parts, axis=0)
    mine = jnp.einsum("ac,amd->cmd", one_hot(got_slots, columns), jnp.concatenate(recv_parts, axis=0),
                      preferred_element_type=jnp.float32).astype(jnp.bfloat16)
    other = swapped(mine)
    return jnp.where(first, jnp.concatenate([mine, other], axis=1),
                     jnp.concatenate([other, mine], axis=1))


def solution(mesh):
    in_specs = (
        P("tile", "chan", None),
        P("chan", None),
        P("tile", "chan"),
        P("tile", None, None),
        P("tile", None),
        P("tile"),
        P("tile"),
    )
    out_specs = P("tile", None, None)
    return jax.shard_map(
        on_device, mesh=mesh, in_specs=in_specs, out_specs=out_specs, check_vma=False
    )
```

```python
import jax
import jax.numpy as jnp
from jax import lax
from jax.experimental import pallas as pl
from jax.experimental.pallas import tpu as pltpu
from jax.sharding import PartitionSpec as P

SPAN = 4
CAP = 3

NT = (((1,), (1,)), ((), ()))


def passed_along(value, axis, by):
    count = lax.axis_size(axis)
    return lax.ppermute(value, axis, [(i, (i + by) % count) for i in range(count)])


def swapped(value):
    return lax.ppermute(value, "chan", [(0, 1), (1, 0)])


def one_hot(index, size):
    return (index[:, None] == jnp.arange(size, dtype=jnp.int32)[None, :]).astype(jnp.bfloat16)


def adjoint_kernel(place_ref, count_ref, s0_ref, s1_ref, s2_ref, s3_ref, jc_ref, jo_ref, ic_ref, io_ref,
                   rcc_ref, rco_ref, roc_ref, roo_ref, out_ref):
    parts = (s0_ref, s1_ref, s2_ref, s3_ref)
    foot = out_ref.shape[0]
    for f in range(foot):
        group = place_ref[f] // CAP
        rank = place_ref[f] % CAP
        s = parts[3][rank]
        for g in (2, 1, 0):
            s = jnp.where(group == g, parts[g][rank], s)
        jc = jc_ref[:, f, :]
        jo = jo_ref[:, f, :]
        ev_c = lax.dot_general(s, jc, NT, preferred_element_type=jnp.float32)
        ev_o = lax.dot_general(s, jo, NT, preferred_element_type=jnp.float32)
        dep_c = (ev_c - ic_ref[f:f + 1, :]).astype(jnp.bfloat16)
        dep_o = (ev_o - io_ref[f:f + 1, :]).astype(jnp.bfloat16)
        w_c = (jnp.dot(dep_c, rcc_ref[...], preferred_element_type=jnp.float32)
               + jnp.dot(dep_o, roc_ref[...], preferred_element_type=jnp.float32)).astype(jnp.bfloat16)
        w_o = (jnp.dot(dep_c, rco_ref[...], preferred_element_type=jnp.float32)
               + jnp.dot(dep_o, roo_ref[...], preferred_element_type=jnp.float32)).astype(jnp.bfloat16)
        adj = (jnp.dot(w_c, jc, preferred_element_type=jnp.float32)
               + jnp.dot(w_o, jo, preferred_element_type=jnp.float32))
        live = f < count_ref[0]
        out_ref[f] = jnp.where(live, adj, 0.0).astype(out_ref.dtype)


def adjoints(place, count, fetched, jac_c, jac_o, innov_c, innov_o, r_blocks):
    half_ch, foot, state = jac_c.shape
    half_m = fetched[0].shape[1]
    smem = pl.BlockSpec(memory_space=pltpu.SMEM)
    vmem = pl.BlockSpec(memory_space=pltpu.VMEM)
    return pl.pallas_call(
        adjoint_kernel,
        in_specs=[smem, smem] + [vmem] * 12,
        out_specs=vmem,
        out_shape=jax.ShapeDtypeStruct((foot, half_m, state), jnp.bfloat16),
    )(place, count, *fetched, jac_c, jac_o, innov_c, innov_o, *r_blocks)


def on_device(jacobian, r_inverse, innovation, increments, owner_offset, column_slot, foot_counts):
    foot = jacobian.shape[0]
    half_ch = jacobian.shape[1]
    columns = increments.shape[0]
    members = increments.shape[1]
    cores = lax.axis_size("chan")
    half_m = members // cores
    core = lax.axis_index("chan")
    capacity = CAP
    slots_total = SPAN * capacity

    jac_c = jnp.transpose(jacobian, (1, 0, 2))
    jac_o = jnp.transpose(swapped(jacobian), (1, 0, 2))
    innov_c = innovation.astype(jnp.float32)
    innov_o = swapped(innovation).astype(jnp.float32)
    r_o = swapped(r_inverse)
    first = core == 0
    rows_lo = jnp.where(first, r_inverse, r_o)
    rows_hi = jnp.where(first, r_o, r_inverse)
    r00, r01 = rows_lo[:, :half_ch], rows_lo[:, half_ch:]
    r10, r11 = rows_hi[:, :half_ch], rows_hi[:, half_ch:]
    r_blocks = (
        jnp.where(first, r00, r11),
        jnp.where(first, r01, r10),
        jnp.where(first, r10, r01),
        jnp.where(first, r11, r00),
    )

    offset = owner_offset[:, 0]
    order = jnp.arange(foot, dtype=jnp.int32)
    earlier = (offset[:, None] == offset[None, :]) & (order[None, :] < order[:, None])
    rank = jnp.sum(earlier.astype(jnp.int32), axis=1)
    place = offset * capacity + rank
    hit = place[None, :] == jnp.arange(slots_total, dtype=jnp.int32)[:, None]
    request = jnp.sum(jnp.where(hit, column_slot[None, :], 0), axis=1)

    own_inc = lax.dynamic_slice_in_dim(increments, core * half_m, half_m, axis=1)

    def pick(index):
        return jnp.einsum("ac,cms->ams", one_hot(index, columns), own_inc,
                          preferred_element_type=jnp.float32).astype(jnp.bfloat16)

    slot_parts = []
    for g in range(SPAN):
        wanted = request[g * capacity:(g + 1) * capacity]
        slot_parts.append(wanted if g == 1 else passed_along(wanted, "tile", g - 1))
    fetched_parts = []
    for g in range(SPAN):
        picked = pick(slot_parts[g])
        fetched_parts.append(picked if g == 1 else passed_along(picked, "tile", 1 - g))
    adjoint = adjoints(place, foot_counts, fetched_parts, jac_c, jac_o, innov_c, innov_o, r_blocks)

    packed = jnp.einsum("af,fmd->amd", hit.astype(jnp.bfloat16), adjoint,
                        preferred_element_type=jnp.float32).astype(jnp.bfloat16)
    recv_parts = []
    for g in range(SPAN):
        piece = packed[g * capacity:(g + 1) * capacity]
        if g == 1:
            recv_parts.append(piece)
        else:
            recv_parts.append(passed_along(piece, "tile", g - 1))
    got_slots = jnp.concatenate(slot_parts, axis=0)
    mine = jnp.einsum("ac,amd->cmd", one_hot(got_slots, columns), jnp.concatenate(recv_parts, axis=0),
                      preferred_element_type=jnp.float32).astype(jnp.bfloat16)
    other = swapped(mine)
    return jnp.where(first, jnp.concatenate([mine, other], axis=1),
                     jnp.concatenate([other, mine], axis=1))


def solution(mesh):
    in_specs = (
        P("tile", "chan", None),
        P("chan", None),
        P("tile", "chan"),
        P("tile", None, None),
        P("tile", None),
        P("tile"),
        P("tile"),
    )
    out_specs = P("tile", None, None)
    return jax.shard_map(
        on_device, mesh=mesh, in_specs=in_specs, out_specs=out_specs, check_vma=False
    )
```

```python
import jax
import jax.numpy as jnp
from jax import lax
from jax.experimental import pallas as pl
from jax.experimental.pallas import tpu as pltpu
from jax.sharding import PartitionSpec as P

SPAN = 4
CAP = 3

NT = (((1,), (1,)), ((), ()))


def passed_along(value, axis, by):
    count = lax.axis_size(axis)
    return lax.ppermute(value, axis, [(i, (i + by) % count) for i in range(count)])


def swapped(value):
    return lax.ppermute(value, "chan", [(0, 1), (1, 0)])


def one_hot(index, size):
    return (index[:, None] == jnp.arange(size, dtype=jnp.int32)[None, :]).astype(jnp.bfloat16)


def adjoint_kernel(place_ref, count_ref, s0_ref, s1_ref, s2_ref, s3_ref, jc_ref, jo_ref, ic_ref, io_ref,
                   rcc_ref, rco_ref, roc_ref, roo_ref, out_ref):
    parts = (s0_ref, s1_ref, s2_ref, s3_ref)
    foot = out_ref.shape[0]
    jcs, jos, deps_c, deps_o = [], [], [], []
    for f in range(foot):
        group = place_ref[f] // CAP
        rank = place_ref[f] % CAP
        s = parts[3][rank]
        for g in (2, 1, 0):
            s = jnp.where(group == g, parts[g][rank], s)
        jc = jc_ref[:, f, :]
        jo = jo_ref[:, f, :]
        jcs.append(jc)
        jos.append(jo)
        ev_c = lax.dot_general(s, jc, NT, preferred_element_type=jnp.float32)
        ev_o = lax.dot_general(s, jo, NT, preferred_element_type=jnp.float32)
        deps_c.append((ev_c - ic_ref[f:f + 1, :]).astype(jnp.bfloat16))
        deps_o.append((ev_o - io_ref[f:f + 1, :]).astype(jnp.bfloat16))
    dep_c = jnp.concatenate(deps_c, axis=0)
    dep_o = jnp.concatenate(deps_o, axis=0)
    w_c = (jnp.dot(dep_c, rcc_ref[...], preferred_element_type=jnp.float32)
           + jnp.dot(dep_o, roc_ref[...], preferred_element_type=jnp.float32)).astype(jnp.bfloat16)
    w_o = (jnp.dot(dep_c, rco_ref[...], preferred_element_type=jnp.float32)
           + jnp.dot(dep_o, roo_ref[...], preferred_element_type=jnp.float32)).astype(jnp.bfloat16)
    rows = deps_c[0].shape[0]
    for f in range(foot):
        adj = (jnp.dot(w_c[f * rows:(f + 1) * rows], jcs[f], preferred_element_type=jnp.float32)
               + jnp.dot(w_o[f * rows:(f + 1) * rows], jos[f], preferred_element_type=jnp.float32))
        live = f < count_ref[0]
        out_ref[f] = jnp.where(live, adj, 0.0).astype(out_ref.dtype)


def adjoints(place, count, fetched, jac_c, jac_o, innov_c, innov_o, r_blocks):
    half_ch, foot, state = jac_c.shape
    half_m = fetched[0].shape[1]
    smem = pl.BlockSpec(memory_space=pltpu.SMEM)
    vmem = pl.BlockSpec(memory_space=pltpu.VMEM)
    return pl.pallas_call(
        adjoint_kernel,
        in_specs=[smem, smem] + [vmem] * 12,
        out_specs=vmem,
        out_shape=jax.ShapeDtypeStruct((foot, half_m, state), jnp.bfloat16),
    )(place, count, *fetched, jac_c, jac_o, innov_c, innov_o, *r_blocks)


def on_device(jacobian, r_inverse, innovation, increments, owner_offset, column_slot, foot_counts):
    foot = jacobian.shape[0]
    half_ch = jacobian.shape[1]
    columns = increments.shape[0]
    members = increments.shape[1]
    cores = lax.axis_size("chan")
    half_m = members // cores
    core = lax.axis_index("chan")
    capacity = CAP
    slots_total = SPAN * capacity

    jac_c = jnp.transpose(jacobian, (1, 0, 2))
    jac_o = jnp.transpose(swapped(jacobian), (1, 0, 2))
    innov_c = innovation.astype(jnp.float32)
    innov_o = swapped(innovation).astype(jnp.float32)
    r_o = swapped(r_inverse)
    first = core == 0
    rows_lo = jnp.where(first, r_inverse, r_o)
    rows_hi = jnp.where(first, r_o, r_inverse)
    r00, r01 = rows_lo[:, :half_ch], rows_lo[:, half_ch:]
    r10, r11 = rows_hi[:, :half_ch], rows_hi[:, half_ch:]
    r_blocks = (
        jnp.where(first, r00, r11),
        jnp.where(first, r01, r10),
        jnp.where(first, r10, r01),
        jnp.where(first, r11, r00),
    )

    offset = owner_offset[:, 0]
    order = jnp.arange(foot, dtype=jnp.int32)
    earlier = (offset[:, None] == offset[None, :]) & (order[None, :] < order[:, None])
    rank = jnp.sum(earlier.astype(jnp.int32), axis=1)
    place = offset * capacity + rank
    hit = place[None, :] == jnp.arange(slots_total, dtype=jnp.int32)[:, None]
    request = jnp.sum(jnp.where(hit, column_slot[None, :], 0), axis=1)

    own_inc = lax.dynamic_slice_in_dim(increments, core * half_m, half_m, axis=1)

    def pick(index):
        return jnp.einsum("ac,cms->ams", one_hot(index, columns), own_inc,
                          preferred_element_type=jnp.float32).astype(jnp.bfloat16)

    slot_parts = []
    for g in range(SPAN):
        wanted = request[g * capacity:(g + 1) * capacity]
        slot_parts.append(wanted if g == 1 else passed_along(wanted, "tile", g - 1))
    fetched_parts = []
    for g in range(SPAN):
        picked = pick(slot_parts[g])
        fetched_parts.append(picked if g == 1 else passed_along(picked, "tile", 1 - g))
    adjoint = adjoints(place, foot_counts, fetched_parts, jac_c, jac_o, innov_c, innov_o, r_blocks)

    packed = jnp.einsum("af,fmd->amd", hit.astype(jnp.bfloat16), adjoint,
                        preferred_element_type=jnp.float32).astype(jnp.bfloat16)
    recv_parts = []
    for g in range(SPAN):
        piece = packed[g * capacity:(g + 1) * capacity]
        if g == 1:
            recv_parts.append(piece)
        else:
            recv_parts.append(passed_along(piece, "tile", g - 1))
    got_slots = jnp.concatenate(slot_parts, axis=0)
    mine = jnp.einsum("ac,amd->cmd", one_hot(got_slots, columns), jnp.concatenate(recv_parts, axis=0),
                      preferred_element_type=jnp.float32).astype(jnp.bfloat16)
    other = swapped(mine)
    return jnp.where(first, jnp.concatenate([mine, other], axis=1),
                     jnp.concatenate([other, mine], axis=1))


def solution(mesh):
    in_specs = (
        P("tile", "chan", None),
        P("chan", None),
        P("tile", "chan"),
        P("tile", None, None),
        P("tile", None),
        P("tile"),
        P("tile"),
    )
    out_specs = P("tile", None, None)
    return jax.shard_map(
        on_device, mesh=mesh, in_specs=in_specs, out_specs=out_specs, check_vma=False
    )
```

```python
import jax
import jax.numpy as jnp
from jax import lax
from jax.experimental import pallas as pl
from jax.experimental.pallas import tpu as pltpu
from jax.sharding import PartitionSpec as P

SPAN = 4
CAP = 3

NT = (((1,), (1,)), ((), ()))


def passed_along(value, axis, by):
    count = lax.axis_size(axis)
    return lax.ppermute(value, axis, [(i, (i + by) % count) for i in range(count)])


def swapped(value):
    return lax.ppermute(value, "chan", [(0, 1), (1, 0)])


def one_hot(index, size):
    return (index[:, None] == jnp.arange(size, dtype=jnp.int32)[None, :]).astype(jnp.bfloat16)


def adjoint_kernel(place_ref, count_ref, s0_ref, s1_ref, s2_ref, s3_ref, jc_ref, jo_ref, ic_ref, io_ref,
                   rcc_ref, rco_ref, roc_ref, roo_ref, out_ref):
    parts = (s0_ref, s1_ref, s2_ref, s3_ref)
    foot = out_ref.shape[0]
    jcs, jos, deps_c, deps_o = [], [], [], []
    for f in range(foot):
        group = place_ref[f] // CAP
        rank = place_ref[f] % CAP
        s = parts[3][rank]
        for g in (2, 1, 0):
            s = jnp.where(group == g, parts[g][rank], s)
        jc = jc_ref[:, f, :]
        jo = jo_ref[:, f, :]
        jcs.append(jc)
        jos.append(jo)
        ev_c = lax.dot_general(s, jc, NT, preferred_element_type=jnp.float32)
        ev_o = lax.dot_general(s, jo, NT, preferred_element_type=jnp.float32)
        deps_c.append((ev_c - ic_ref[f:f + 1, :]).astype(jnp.bfloat16))
        deps_o.append((ev_o - io_ref[f:f + 1, :]).astype(jnp.bfloat16))
    dep_c = jnp.concatenate(deps_c, axis=0)
    dep_o = jnp.concatenate(deps_o, axis=0)
    w_c = (jnp.dot(dep_c, rcc_ref[...], preferred_element_type=jnp.float32)
           + jnp.dot(dep_o, roc_ref[...], preferred_element_type=jnp.float32)).astype(jnp.bfloat16)
    w_o = (jnp.dot(dep_c, rco_ref[...], preferred_element_type=jnp.float32)
           + jnp.dot(dep_o, roo_ref[...], preferred_element_type=jnp.float32)).astype(jnp.bfloat16)
    rows = deps_c[0].shape[0]
    for f in range(foot):
        adj = (jnp.dot(w_c[f * rows:(f + 1) * rows], jcs[f], preferred_element_type=jnp.float32)
               + jnp.dot(w_o[f * rows:(f + 1) * rows], jos[f], preferred_element_type=jnp.float32))
        live = f < count_ref[0]
        out_ref[f] = jnp.where(live, adj, 0.0).astype(out_ref.dtype)


def adjoints(place, count, fetched, jac_c, jac_o, innov_c, innov_o, r_blocks):
    half_ch, foot, state = jac_c.shape
    half_m = fetched[0].shape[1]
    smem = pl.BlockSpec(memory_space=pltpu.SMEM)
    vmem = pl.BlockSpec(memory_space=pltpu.VMEM)
    return pl.pallas_call(
        adjoint_kernel,
        in_specs=[smem, smem] + [vmem] * 12,
        out_specs=vmem,
        out_shape=jax.ShapeDtypeStruct((foot, half_m, state), jnp.bfloat16),
    )(place, count, *fetched, jac_c, jac_o, innov_c, innov_o, *r_blocks)


def on_device(jacobian, r_inverse, innovation, increments, owner_offset, column_slot, foot_counts):
    foot = jacobian.shape[0]
    half_ch = jacobian.shape[1]
    columns = increments.shape[0]
    members = increments.shape[1]
    cores = lax.axis_size("chan")
    half_m = members // cores
    core = lax.axis_index("chan")
    capacity = CAP
    slots_total = SPAN * capacity

    jac_c = jnp.transpose(jacobian, (1, 0, 2))
    innov_c = innovation.astype(jnp.float32)
    innov_o = swapped(innovation).astype(jnp.float32)
    r_o = swapped(r_inverse)
    first = core == 0
    rows_lo = jnp.where(first, r_inverse, r_o)
    rows_hi = jnp.where(first, r_o, r_inverse)
    r00, r01 = rows_lo[:, :half_ch], rows_lo[:, half_ch:]
    r10, r11 = rows_hi[:, :half_ch], rows_hi[:, half_ch:]
    r_blocks = (
        jnp.where(first, r00, r11),
        jnp.where(first, r01, r10),
        jnp.where(first, r10, r01),
        jnp.where(first, r11, r00),
    )

    offset = owner_offset[:, 0]
    order = jnp.arange(foot, dtype=jnp.int32)
    earlier = (offset[:, None] == offset[None, :]) & (order[None, :] < order[:, None])
    rank = jnp.sum(earlier.astype(jnp.int32), axis=1)
    place = offset * capacity + rank
    hit = place[None, :] == jnp.arange(slots_total, dtype=jnp.int32)[:, None]
    request = jnp.sum(jnp.where(hit, column_slot[None, :], 0), axis=1)

    own_inc = lax.dynamic_slice_in_dim(increments, core * half_m, half_m, axis=1)

    def pick(index):
        return jnp.einsum("ac,cms->ams", one_hot(index, columns), own_inc,
                          preferred_element_type=jnp.float32).astype(jnp.bfloat16)

    slot_parts = []
    for g in range(SPAN):
        wanted = request[g * capacity:(g + 1) * capacity]
        slot_parts.append(wanted if g == 1 else passed_along(wanted, "tile", g - 1))
    slot_parts, held = lax.optimization_barrier((slot_parts, jacobian))
    jac_o = jnp.transpose(swapped(held), (1, 0, 2))
    fetched_parts = []
    for g in range(SPAN):
        picked = pick(slot_parts[g])
        fetched_parts.append(picked if g == 1 else passed_along(picked, "tile", 1 - g))
    adjoint = adjoints(place, foot_counts, fetched_parts, jac_c, jac_o, innov_c, innov_o, r_blocks)

    packed = jnp.einsum("af,fmd->amd", hit.astype(jnp.bfloat16), adjoint,
                        preferred_element_type=jnp.float32).astype(jnp.bfloat16)
    recv_parts = []
    for g in range(SPAN):
        piece = packed[g * capacity:(g + 1) * capacity]
        if g == 1:
            recv_parts.append(piece)
        else:
            recv_parts.append(passed_along(piece, "tile", g - 1))
    got_slots = jnp.concatenate(slot_parts, axis=0)
    mine = jnp.einsum("ac,amd->cmd", one_hot(got_slots, columns), jnp.concatenate(recv_parts, axis=0),
                      preferred_element_type=jnp.float32).astype(jnp.bfloat16)
    other = swapped(mine)
    return jnp.where(first, jnp.concatenate([mine, other], axis=1),
                     jnp.concatenate([other, mine], axis=1))


def solution(mesh):
    in_specs = (
        P("tile", "chan", None),
        P("chan", None),
        P("tile", "chan"),
        P("tile", None, None),
        P("tile", None),
        P("tile"),
        P("tile"),
    )
    out_specs = P("tile", None, None)
    return jax.shard_map(
        on_device, mesh=mesh, in_specs=in_specs, out_specs=out_specs, check_vma=False
    )
```

```python
import jax
import jax.numpy as jnp
from jax import lax
from jax.experimental import pallas as pl
from jax.experimental.pallas import tpu as pltpu
from jax.sharding import PartitionSpec as P

SPAN = 4
CAP = 3

NT = (((1,), (1,)), ((), ()))


def passed_along(value, axis, by):
    count = lax.axis_size(axis)
    return lax.ppermute(value, axis, [(i, (i + by) % count) for i in range(count)])


def swapped(value):
    return lax.ppermute(value, "chan", [(0, 1), (1, 0)])


def one_hot(index, size):
    return (index[:, None] == jnp.arange(size, dtype=jnp.int32)[None, :]).astype(jnp.bfloat16)


def adjoint_kernel(place_ref, count_ref, s0_ref, s1_ref, s2_ref, s3_ref, jc_ref, jo_ref, ic_ref, io_ref,
                   rcc_ref, rco_ref, roc_ref, roo_ref, o0_ref, o1_ref, o2_ref, o3_ref):
    outs = (o0_ref, o1_ref, o2_ref, o3_ref)
    parts = (s0_ref, s1_ref, s2_ref, s3_ref)
    foot = jc_ref.shape[1]
    jcs, jos, deps_c, deps_o = [], [], [], []
    for f in range(foot):
        group = place_ref[f] // CAP
        rank = place_ref[f] % CAP
        s = parts[3][rank]
        for g in (2, 1, 0):
            s = jnp.where(group == g, parts[g][rank], s)
        jc = jc_ref[:, f, :]
        jo = jo_ref[:, f, :]
        jcs.append(jc)
        jos.append(jo)
        ev_c = lax.dot_general(s, jc, NT, preferred_element_type=jnp.float32)
        ev_o = lax.dot_general(s, jo, NT, preferred_element_type=jnp.float32)
        deps_c.append((ev_c - ic_ref[f:f + 1, :]).astype(jnp.bfloat16))
        deps_o.append((ev_o - io_ref[f:f + 1, :]).astype(jnp.bfloat16))
    dep_c = jnp.concatenate(deps_c, axis=0)
    dep_o = jnp.concatenate(deps_o, axis=0)
    w_c = (jnp.dot(dep_c, rcc_ref[...], preferred_element_type=jnp.float32)
           + jnp.dot(dep_o, roc_ref[...], preferred_element_type=jnp.float32)).astype(jnp.bfloat16)
    w_o = (jnp.dot(dep_c, rco_ref[...], preferred_element_type=jnp.float32)
           + jnp.dot(dep_o, roo_ref[...], preferred_element_type=jnp.float32)).astype(jnp.bfloat16)
    rows = deps_c[0].shape[0]
    for o_ref in outs:
        o_ref[...] = jnp.zeros(o_ref.shape, o_ref.dtype)
    for f in range(foot):
        adj = (jnp.dot(w_c[f * rows:(f + 1) * rows], jcs[f], preferred_element_type=jnp.float32)
               + jnp.dot(w_o[f * rows:(f + 1) * rows], jos[f], preferred_element_type=jnp.float32))
        live = f < count_ref[0]
        adj = jnp.where(live, adj, 0.0).astype(jnp.bfloat16)
        group = place_ref[f] // CAP
        rank = place_ref[f] % CAP
        for g in range(SPAN):
            @pl.when(group == g)
            def _():
                outs[g][rank] = adj


def adjoints(place, count, fetched, jac_c, jac_o, innov_c, innov_o, r_blocks):
    half_ch, foot, state = jac_c.shape
    half_m = fetched[0].shape[1]
    smem = pl.BlockSpec(memory_space=pltpu.SMEM)
    vmem = pl.BlockSpec(memory_space=pltpu.VMEM)
    return pl.pallas_call(
        adjoint_kernel,
        in_specs=[smem, smem] + [vmem] * 12,
        out_specs=[vmem] * SPAN,
        out_shape=[jax.ShapeDtypeStruct((CAP, half_m, state), jnp.bfloat16)] * SPAN,
    )(place, count, *fetched, jac_c, jac_o, innov_c, innov_o, *r_blocks)


def on_device(jacobian, r_inverse, innovation, increments, owner_offset, column_slot, foot_counts):
    foot = jacobian.shape[0]
    half_ch = jacobian.shape[1]
    columns = increments.shape[0]
    members = increments.shape[1]
    cores = lax.axis_size("chan")
    half_m = members // cores
    core = lax.axis_index("chan")
    capacity = CAP
    slots_total = SPAN * capacity

    jac_c = jnp.transpose(jacobian, (1, 0, 2))
    jac_o = jnp.transpose(swapped(jacobian), (1, 0, 2))
    innov_c = innovation.astype(jnp.float32)
    innov_o = swapped(innovation).astype(jnp.float32)
    r_o = swapped(r_inverse)
    first = core == 0
    rows_lo = jnp.where(first, r_inverse, r_o)
    rows_hi = jnp.where(first, r_o, r_inverse)
    r00, r01 = rows_lo[:, :half_ch], rows_lo[:, half_ch:]
    r10, r11 = rows_hi[:, :half_ch], rows_hi[:, half_ch:]
    r_blocks = (
        jnp.where(first, r00, r11),
        jnp.where(first, r01, r10),
        jnp.where(first, r10, r01),
        jnp.where(first, r11, r00),
    )

    offset = owner_offset[:, 0]
    order = jnp.arange(foot, dtype=jnp.int32)
    earlier = (offset[:, None] == offset[None, :]) & (order[None, :] < order[:, None])
    rank = jnp.sum(earlier.astype(jnp.int32), axis=1)
    place = offset * capacity + rank
    hit = place[None, :] == jnp.arange(slots_total, dtype=jnp.int32)[:, None]
    request = jnp.sum(jnp.where(hit, column_slot[None, :], 0), axis=1)

    own_inc = lax.dynamic_slice_in_dim(increments, core * half_m, half_m, axis=1)

    def pick(index):
        return jnp.einsum("ac,cms->ams", one_hot(index, columns), own_inc,
                          preferred_element_type=jnp.float32).astype(jnp.bfloat16)

    slot_parts = []
    for g in range(SPAN):
        wanted = request[g * capacity:(g + 1) * capacity]
        slot_parts.append(wanted if g == 1 else passed_along(wanted, "tile", g - 1))
    fetched_parts = []
    for g in range(SPAN):
        picked = pick(slot_parts[g])
        fetched_parts.append(picked if g == 1 else passed_along(picked, "tile", 1 - g))
    packed = adjoints(place, foot_counts, fetched_parts, jac_c, jac_o, innov_c, innov_o, r_blocks)
    recv_parts = []
    for g in range(SPAN):
        piece = packed[g]
        if g == 1:
            recv_parts.append(piece)
        else:
            recv_parts.append(passed_along(piece, "tile", g - 1))
    got_slots = jnp.concatenate(slot_parts, axis=0)
    mine = jnp.einsum("ac,amd->cmd", one_hot(got_slots, columns), jnp.concatenate(recv_parts, axis=0),
                      preferred_element_type=jnp.float32).astype(jnp.bfloat16)
    other = swapped(mine)
    return jnp.where(first, jnp.concatenate([mine, other], axis=1),
                     jnp.concatenate([other, mine], axis=1))


def solution(mesh):
    in_specs = (
        P("tile", "chan", None),
        P("chan", None),
        P("tile", "chan"),
        P("tile", None, None),
        P("tile", None),
        P("tile"),
        P("tile"),
    )
    out_specs = P("tile", None, None)
    return jax.shard_map(
        on_device, mesh=mesh, in_specs=in_specs, out_specs=out_specs, check_vma=False
    )
```

```python
import jax
import jax.numpy as jnp
from jax import lax
from jax.experimental import pallas as pl
from jax.experimental.pallas import tpu as pltpu
from jax.sharding import PartitionSpec as P

SPAN = 4
CAP = 3

NT = (((1,), (1,)), ((), ()))


def passed_along(value, axis, by):
    count = lax.axis_size(axis)
    return lax.ppermute(value, axis, [(i, (i + by) % count) for i in range(count)])


def swapped(value):
    return lax.ppermute(value, "chan", [(0, 1), (1, 0)])


def one_hot(index, size):
    return (index[:, None] == jnp.arange(size, dtype=jnp.int32)[None, :]).astype(jnp.bfloat16)


def adjoint_kernel(place_ref, count_ref, s0_ref, s1_ref, s2_ref, s3_ref, jc_ref, jo_ref, ic_ref, io_ref,
                   rcc_ref, rco_ref, roc_ref, roo_ref, o0_ref, o1_ref, o2_ref, o3_ref,
                   jc_s, jo_s, dc_s, do_s):
    parts = (s0_ref, s1_ref, s2_ref, s3_ref)
    outs = (o0_ref, o1_ref, o2_ref, o3_ref)
    foot = jc_s.shape[0]
    rows = s0_ref.shape[1]
    f = pl.program_id(0)
    group = place_ref[f] // CAP
    rank = place_ref[f] % CAP
    s = parts[3][rank]
    for g in (2, 1, 0):
        s = jnp.where(group == g, parts[g][rank], s)
    jc = jc_ref[0]
    jo = jo_ref[0]
    jc_s[f] = jc
    jo_s[f] = jo
    ev_c = lax.dot_general(s, jc, NT, preferred_element_type=jnp.float32)
    ev_o = lax.dot_general(s, jo, NT, preferred_element_type=jnp.float32)
    at = pl.multiple_of(f * rows, rows)
    dc_s[pl.ds(at, rows), :] = (ev_c - ic_ref[pl.ds(f, 1), :]).astype(jnp.bfloat16)
    do_s[pl.ds(at, rows), :] = (ev_o - io_ref[pl.ds(f, 1), :]).astype(jnp.bfloat16)

    @pl.when(f == foot - 1)
    def _():
        dep_c = dc_s[...]
        dep_o = do_s[...]
        w_c = (jnp.dot(dep_c, rcc_ref[...], preferred_element_type=jnp.float32)
               + jnp.dot(dep_o, roc_ref[...], preferred_element_type=jnp.float32)).astype(jnp.bfloat16)
        w_o = (jnp.dot(dep_c, rco_ref[...], preferred_element_type=jnp.float32)
               + jnp.dot(dep_o, roo_ref[...], preferred_element_type=jnp.float32)).astype(jnp.bfloat16)
        for o_ref in outs:
            o_ref[...] = jnp.zeros(o_ref.shape, o_ref.dtype)
        for h in range(foot):
            adj = (jnp.dot(w_c[h * rows:(h + 1) * rows], jc_s[h], preferred_element_type=jnp.float32)
                   + jnp.dot(w_o[h * rows:(h + 1) * rows], jo_s[h], preferred_element_type=jnp.float32))
            adj = jnp.where(h < count_ref[0], adj, 0.0).astype(jnp.bfloat16)
            grp = place_ref[h] // CAP
            rnk = place_ref[h] % CAP
            for g in range(SPAN):
                @pl.when(grp == g)
                def _():
                    outs[g][rnk] = adj


def adjoints(place, count, fetched, jac_c, jac_o, innov_c, innov_o, r_blocks):
    foot, half_ch, state = jac_c.shape
    half_m = fetched[0].shape[1]
    whole3 = lambda f, p, n: (0, 0, 0)
    whole2 = lambda f, p, n: (0, 0)
    part = pl.BlockSpec(fetched[0].shape, whole3)
    jblock = pl.BlockSpec((1, half_ch, state), lambda f, p, n: (f, 0, 0))
    grid_spec = pltpu.PrefetchScalarGridSpec(
        num_scalar_prefetch=2,
        grid=(foot,),
        in_specs=[part] * SPAN + [jblock, jblock,
                                  pl.BlockSpec((foot, half_ch), whole2),
                                  pl.BlockSpec((foot, half_ch), whole2)]
                 + [pl.BlockSpec((half_ch, half_ch), whole2)] * 4,
        out_specs=[pl.BlockSpec((CAP, half_m, state), whole3)] * SPAN,
        scratch_shapes=[pltpu.VMEM((foot, half_ch, state), jnp.bfloat16),
                        pltpu.VMEM((foot, half_ch, state), jnp.bfloat16),
                        pltpu.VMEM((foot * half_m, half_ch), jnp.bfloat16),
                        pltpu.VMEM((foot * half_m, half_ch), jnp.bfloat16)],
    )
    return pl.pallas_call(
        adjoint_kernel,
        grid_spec=grid_spec,
        out_shape=[jax.ShapeDtypeStruct((CAP, half_m, state), jnp.bfloat16)] * SPAN,
    )(place, count, *fetched, jac_c, jac_o, innov_c, innov_o, *r_blocks)


def on_device(jacobian, r_inverse, innovation, increments, owner_offset, column_slot, foot_counts):
    foot = jacobian.shape[0]
    half_ch = jacobian.shape[1]
    columns = increments.shape[0]
    members = increments.shape[1]
    cores = lax.axis_size("chan")
    half_m = members // cores
    core = lax.axis_index("chan")
    capacity = CAP
    slots_total = SPAN * capacity

    jac_c = jacobian
    jac_o = swapped(jacobian)
    innov_c = innovation.astype(jnp.float32)
    innov_o = swapped(innovation).astype(jnp.float32)
    r_o = swapped(r_inverse)
    first = core == 0
    rows_lo = jnp.where(first, r_inverse, r_o)
    rows_hi = jnp.where(first, r_o, r_inverse)
    r00, r01 = rows_lo[:, :half_ch], rows_lo[:, half_ch:]
    r10, r11 = rows_hi[:, :half_ch], rows_hi[:, half_ch:]
    r_blocks = (
        jnp.where(first, r00, r11),
        jnp.where(first, r01, r10),
        jnp.where(first, r10, r01),
        jnp.where(first, r11, r00),
    )

    offset = owner_offset[:, 0]
    order = jnp.arange(foot, dtype=jnp.int32)
    earlier = (offset[:, None] == offset[None, :]) & (order[None, :] < order[:, None])
    rank = jnp.sum(earlier.astype(jnp.int32), axis=1)
    place = offset * capacity + rank
    hit = place[None, :] == jnp.arange(slots_total, dtype=jnp.int32)[:, None]
    request = jnp.sum(jnp.where(hit, column_slot[None, :], 0), axis=1)

    own_inc = lax.dynamic_slice_in_dim(increments, core * half_m, half_m, axis=1)

    def pick(index):
        return jnp.einsum("ac,cms->ams", one_hot(index, columns), own_inc,
                          preferred_element_type=jnp.float32).astype(jnp.bfloat16)

    slot_parts = []
    for g in range(SPAN):
        wanted = request[g * capacity:(g + 1) * capacity]
        slot_parts.append(wanted if g == 1 else passed_along(wanted, "tile", g - 1))
    fetched_parts = []
    for g in range(SPAN):
        picked = pick(slot_parts[g])
        fetched_parts.append(picked if g == 1 else passed_along(picked, "tile", 1 - g))
    packed = adjoints(place, foot_counts, fetched_parts, jac_c, jac_o, innov_c, innov_o, r_blocks)
    recv_parts = []
    for g in range(SPAN):
        piece = packed[g]
        if g == 1:
            recv_parts.append(piece)
        else:
            recv_parts.append(passed_along(piece, "tile", g - 1))
    got_slots = jnp.concatenate(slot_parts, axis=0)
    mine = jnp.einsum("ac,amd->cmd", one_hot(got_slots, columns), jnp.concatenate(recv_parts, axis=0),
                      preferred_element_type=jnp.float32).astype(jnp.bfloat16)
    other = swapped(mine)
    return jnp.where(first, jnp.concatenate([mine, other], axis=1),
                     jnp.concatenate([other, mine], axis=1))


def solution(mesh):
    in_specs = (
        P("tile", "chan", None),
        P("chan", None),
        P("tile", "chan"),
        P("tile", None, None),
        P("tile", None),
        P("tile"),
        P("tile"),
    )
    out_specs = P("tile", None, None)
    return jax.shard_map(
        on_device, mesh=mesh, in_specs=in_specs, out_specs=out_specs, check_vma=False
    )
```

```python
import jax
import jax.numpy as jnp
from jax import lax
from jax.experimental import pallas as pl
from jax.experimental.pallas import tpu as pltpu
from jax.sharding import PartitionSpec as P

SPAN = 4
CAP = 3

NT = (((1,), (1,)), ((), ()))


def passed_along(value, axis, by):
    count = lax.axis_size(axis)
    return lax.ppermute(value, axis, [(i, (i + by) % count) for i in range(count)])


def swapped(value):
    return lax.ppermute(value, "chan", [(0, 1), (1, 0)])


def one_hot(index, size):
    return (index[:, None] == jnp.arange(size, dtype=jnp.int32)[None, :]).astype(jnp.bfloat16)


def adjoint_kernel(place_ref, count_ref, s0_ref, s1_ref, s2_ref, s3_ref, jc_ref, jo_ref, ic_ref, io_ref,
                   rcc_ref, rco_ref, roc_ref, roo_ref, o0_ref, o1_ref, o2_ref, o3_ref,
                   jc_s, jo_s, dc_s, do_s):
    parts = (s0_ref, s1_ref, s2_ref, s3_ref)
    outs = (o0_ref, o1_ref, o2_ref, o3_ref)
    foot = jc_s.shape[0]
    rows = s0_ref.shape[1]
    f = pl.program_id(0)
    group = place_ref[f] // CAP
    rank = place_ref[f] % CAP
    s = parts[3][rank]
    for g in (2, 1, 0):
        s = jnp.where(group == g, parts[g][rank], s)
    jc = jc_ref[0]
    jo = jo_ref[0]
    jc_s[f] = jc
    jo_s[f] = jo
    ev_c = lax.dot_general(s, jc, NT, preferred_element_type=jnp.float32)
    ev_o = lax.dot_general(s, jo, NT, preferred_element_type=jnp.float32)
    at = pl.multiple_of(f * rows, rows)
    dc_s[pl.ds(at, rows), :] = (ev_c - ic_ref[pl.ds(f, 1), :]).astype(jnp.bfloat16)
    do_s[pl.ds(at, rows), :] = (ev_o - io_ref[pl.ds(f, 1), :]).astype(jnp.bfloat16)

    @pl.when(f == foot - 1)
    def _():
        dep_c = dc_s[...]
        dep_o = do_s[...]
        w_c = (jnp.dot(dep_c, rcc_ref[...], preferred_element_type=jnp.float32)
               + jnp.dot(dep_o, roc_ref[...], preferred_element_type=jnp.float32)).astype(jnp.bfloat16)
        w_o = (jnp.dot(dep_c, rco_ref[...], preferred_element_type=jnp.float32)
               + jnp.dot(dep_o, roo_ref[...], preferred_element_type=jnp.float32)).astype(jnp.bfloat16)
        for o_ref in outs:
            o_ref[...] = jnp.zeros(o_ref.shape, o_ref.dtype)
        for h in range(foot):
            adj = (jnp.dot(w_c[h * rows:(h + 1) * rows], jc_s[h], preferred_element_type=jnp.float32)
                   + jnp.dot(w_o[h * rows:(h + 1) * rows], jo_s[h], preferred_element_type=jnp.float32))
            adj = jnp.where(h < count_ref[0], adj, 0.0).astype(jnp.bfloat16)
            grp = place_ref[h] // CAP
            rnk = place_ref[h] % CAP
            for g in range(SPAN):
                @pl.when(grp == g)
                def _():
                    outs[g][rnk] = adj


def adjoints(place, count, fetched, jac_c, jac_o, innov_c, innov_o, r_blocks):
    foot, half_ch, state = jac_c.shape
    half_m = fetched[0].shape[1]
    whole3 = lambda f, p, n: (0, 0, 0)
    whole2 = lambda f, p, n: (0, 0)
    part = pl.BlockSpec(fetched[0].shape, whole3)
    jblock = pl.BlockSpec((1, half_ch, state), lambda f, p, n: (f, 0, 0))
    grid_spec = pltpu.PrefetchScalarGridSpec(
        num_scalar_prefetch=2,
        grid=(foot,),
        in_specs=[part] * SPAN + [jblock, jblock,
                                  pl.BlockSpec((foot, half_ch), whole2),
                                  pl.BlockSpec((foot, half_ch), whole2)]
                 + [pl.BlockSpec((half_ch, half_ch), whole2)] * 4,
        out_specs=[pl.BlockSpec((CAP, half_m, state), whole3)] * SPAN,
        scratch_shapes=[pltpu.VMEM((foot, half_ch, state), jnp.bfloat16),
                        pltpu.VMEM((foot, half_ch, state), jnp.bfloat16),
                        pltpu.VMEM((foot * half_m, half_ch), jnp.bfloat16),
                        pltpu.VMEM((foot * half_m, half_ch), jnp.bfloat16)],
    )
    return pl.pallas_call(
        adjoint_kernel,
        grid_spec=grid_spec,
        out_shape=[jax.ShapeDtypeStruct((CAP, half_m, state), jnp.bfloat16)] * SPAN,
    )(place, count, *fetched, jac_c, jac_o, innov_c, innov_o, *r_blocks)


def on_device(jacobian, r_inverse, innovation, increments, owner_offset, column_slot, foot_counts):
    foot = jacobian.shape[0]
    half_ch = jacobian.shape[1]
    columns = increments.shape[0]
    members = increments.shape[1]
    cores = lax.axis_size("chan")
    half_m = members // cores
    core = lax.axis_index("chan")
    capacity = CAP
    slots_total = SPAN * capacity

    jac_c = jacobian
    jac_o = swapped(jacobian)
    innov_c = innovation.astype(jnp.float32)
    innov_o = swapped(innovation).astype(jnp.float32)
    r_o = swapped(r_inverse)
    first = core == 0
    rows_lo = jnp.where(first, r_inverse, r_o)
    rows_hi = jnp.where(first, r_o, r_inverse)
    r00, r01 = rows_lo[:, :half_ch], rows_lo[:, half_ch:]
    r10, r11 = rows_hi[:, :half_ch], rows_hi[:, half_ch:]
    r_blocks = (
        jnp.where(first, r00, r11),
        jnp.where(first, r01, r10),
        jnp.where(first, r10, r01),
        jnp.where(first, r11, r00),
    )

    offset = owner_offset[:, 0]
    order = jnp.arange(foot, dtype=jnp.int32)
    earlier = (offset[:, None] == offset[None, :]) & (order[None, :] < order[:, None])
    rank = jnp.sum(earlier.astype(jnp.int32), axis=1)
    place = offset * capacity + rank
    hit = place[None, :] == jnp.arange(slots_total, dtype=jnp.int32)[:, None]
    request = jnp.sum(jnp.where(hit, column_slot[None, :], 0), axis=1)

    own_inc = lax.dynamic_slice_in_dim(increments, core * half_m, half_m, axis=1)

    def pick(index):
        return jnp.einsum("ac,cms->ams", one_hot(index, columns), own_inc,
                          preferred_element_type=jnp.float32).astype(jnp.bfloat16)

    slot_parts = []
    for g in range(SPAN):
        wanted = request[g * capacity:(g + 1) * capacity]
        slot_parts.append(wanted if g == 1 else passed_along(wanted, "tile", g - 1))
    picked = [pick(slot_parts[g]) for g in range(SPAN)]
    picked, jac_c = lax.optimization_barrier((picked, jac_c))
    fetched_parts = [p if g == 1 else passed_along(p, "tile", 1 - g) for g, p in enumerate(picked)]
    packed = adjoints(place, foot_counts, fetched_parts, jac_c, jac_o, innov_c, innov_o, r_blocks)
    recv_parts = []
    for g in range(SPAN):
        piece = packed[g]
        if g == 1:
            recv_parts.append(piece)
        else:
            recv_parts.append(passed_along(piece, "tile", g - 1))
    got_slots = jnp.concatenate(slot_parts, axis=0)
    mine = jnp.einsum("ac,amd->cmd", one_hot(got_slots, columns), jnp.concatenate(recv_parts, axis=0),
                      preferred_element_type=jnp.float32).astype(jnp.bfloat16)
    other = swapped(mine)
    return jnp.where(first, jnp.concatenate([mine, other], axis=1),
                     jnp.concatenate([other, mine], axis=1))


def solution(mesh):
    in_specs = (
        P("tile", "chan", None),
        P("chan", None),
        P("tile", "chan"),
        P("tile", None, None),
        P("tile", None),
        P("tile"),
        P("tile"),
    )
    out_specs = P("tile", None, None)
    return jax.shard_map(
        on_device, mesh=mesh, in_specs=in_specs, out_specs=out_specs, check_vma=False
    )
```

```python
import jax
import jax.numpy as jnp
from jax import lax
from jax.experimental import pallas as pl
from jax.experimental.pallas import tpu as pltpu
from jax.sharding import PartitionSpec as P

SPAN = 4
CAP = 3

NT = (((1,), (1,)), ((), ()))


def passed_along(value, axis, by):
    count = lax.axis_size(axis)
    return lax.ppermute(value, axis, [(i, (i + by) % count) for i in range(count)])


def swapped(value):
    return lax.ppermute(value, "chan", [(0, 1), (1, 0)])


def one_hot(index, size):
    return (index[:, None] == jnp.arange(size, dtype=jnp.int32)[None, :]).astype(jnp.bfloat16)


def adjoint_kernel(place_ref, count_ref, s0_ref, s1_ref, s2_ref, s3_ref, jc_ref, jo_ref, ic_ref, io_ref,
                   rcc_ref, rco_ref, roc_ref, roo_ref, o0_ref, o1_ref, o2_ref, o3_ref,
                   jc_s, jo_s, dc_s, do_s):
    parts = (s0_ref, s1_ref, s2_ref, s3_ref)
    outs = (o0_ref, o1_ref, o2_ref, o3_ref)
    foot = jc_s.shape[0]
    rows = s0_ref.shape[1]
    f = pl.program_id(0)
    group = place_ref[f] // CAP
    rank = place_ref[f] % CAP
    s = parts[3][rank]
    for g in (2, 1, 0):
        s = jnp.where(group == g, parts[g][rank], s)
    @pl.when(f == 0)
    def _():
        for h in range(foot):
            jc_s[h] = jc_ref[:, h, :]

    jc = jc_s[f]
    jo = jo_ref[0]
    jo_s[f] = jo
    ev_c = lax.dot_general(s, jc, NT, preferred_element_type=jnp.float32)
    ev_o = lax.dot_general(s, jo, NT, preferred_element_type=jnp.float32)
    at = pl.multiple_of(f * rows, rows)
    dc_s[pl.ds(at, rows), :] = (ev_c - ic_ref[pl.ds(f, 1), :]).astype(jnp.bfloat16)
    do_s[pl.ds(at, rows), :] = (ev_o - io_ref[pl.ds(f, 1), :]).astype(jnp.bfloat16)

    @pl.when(f == foot - 1)
    def _():
        dep_c = dc_s[...]
        dep_o = do_s[...]
        w_c = (jnp.dot(dep_c, rcc_ref[...], preferred_element_type=jnp.float32)
               + jnp.dot(dep_o, roc_ref[...], preferred_element_type=jnp.float32)).astype(jnp.bfloat16)
        w_o = (jnp.dot(dep_c, rco_ref[...], preferred_element_type=jnp.float32)
               + jnp.dot(dep_o, roo_ref[...], preferred_element_type=jnp.float32)).astype(jnp.bfloat16)
        for o_ref in outs:
            o_ref[...] = jnp.zeros(o_ref.shape, o_ref.dtype)
        for h in range(foot):
            adj = (jnp.dot(w_c[h * rows:(h + 1) * rows], jc_s[h], preferred_element_type=jnp.float32)
                   + jnp.dot(w_o[h * rows:(h + 1) * rows], jo_s[h], preferred_element_type=jnp.float32))
            adj = jnp.where(h < count_ref[0], adj, 0.0).astype(jnp.bfloat16)
            grp = place_ref[h] // CAP
            rnk = place_ref[h] % CAP
            for g in range(SPAN):
                @pl.when(grp == g)
                def _():
                    outs[g][rnk] = adj


def adjoints(place, count, fetched, jac_c, jac_o, innov_c, innov_o, r_blocks):
    half_ch, foot, state = jac_c.shape
    half_m = fetched[0].shape[1]
    whole3 = lambda f, p, n: (0, 0, 0)
    whole2 = lambda f, p, n: (0, 0)
    part = pl.BlockSpec(fetched[0].shape, whole3)
    jblock = pl.BlockSpec((1, half_ch, state), lambda f, p, n: (f, 0, 0))
    grid_spec = pltpu.PrefetchScalarGridSpec(
        num_scalar_prefetch=2,
        grid=(foot,),
        in_specs=[part] * SPAN + [pl.BlockSpec((half_ch, foot, state), whole3), jblock,
                                  pl.BlockSpec((foot, half_ch), whole2),
                                  pl.BlockSpec((foot, half_ch), whole2)]
                 + [pl.BlockSpec((half_ch, half_ch), whole2)] * 4,
        out_specs=[pl.BlockSpec((CAP, half_m, state), whole3)] * SPAN,
        scratch_shapes=[pltpu.VMEM((foot, half_ch, state), jnp.bfloat16),
                        pltpu.VMEM((foot, half_ch, state), jnp.bfloat16),
                        pltpu.VMEM((foot * half_m, half_ch), jnp.bfloat16),
                        pltpu.VMEM((foot * half_m, half_ch), jnp.bfloat16)],
    )
    return pl.pallas_call(
        adjoint_kernel,
        grid_spec=grid_spec,
        out_shape=[jax.ShapeDtypeStruct((CAP, half_m, state), jnp.bfloat16)] * SPAN,
    )(place, count, *fetched, jac_c, jac_o, innov_c, innov_o, *r_blocks)


def on_device(jacobian, r_inverse, innovation, increments, owner_offset, column_slot, foot_counts):
    foot = jacobian.shape[0]
    half_ch = jacobian.shape[1]
    columns = increments.shape[0]
    members = increments.shape[1]
    cores = lax.axis_size("chan")
    half_m = members // cores
    core = lax.axis_index("chan")
    capacity = CAP
    slots_total = SPAN * capacity

    jac_c = jnp.transpose(jacobian, (1, 0, 2))
    jac_o = swapped(jacobian)
    innov_c = innovation.astype(jnp.float32)
    innov_o = swapped(innovation).astype(jnp.float32)
    r_o = swapped(r_inverse)
    first = core == 0
    rows_lo = jnp.where(first, r_inverse, r_o)
    rows_hi = jnp.where(first, r_o, r_inverse)
    r00, r01 = rows_lo[:, :half_ch], rows_lo[:, half_ch:]
    r10, r11 = rows_hi[:, :half_ch], rows_hi[:, half_ch:]
    r_blocks = (
        jnp.where(first, r00, r11),
        jnp.where(first, r01, r10),
        jnp.where(first, r10, r01),
        jnp.where(first, r11, r00),
    )

    offset = owner_offset[:, 0]
    order = jnp.arange(foot, dtype=jnp.int32)
    earlier = (offset[:, None] == offset[None, :]) & (order[None, :] < order[:, None])
    rank = jnp.sum(earlier.astype(jnp.int32), axis=1)
    place = offset * capacity + rank
    hit = place[None, :] == jnp.arange(slots_total, dtype=jnp.int32)[:, None]
    request = jnp.sum(jnp.where(hit, column_slot[None, :], 0), axis=1)

    own_inc = lax.dynamic_slice_in_dim(increments, core * half_m, half_m, axis=1)

    def pick(index):
        return jnp.einsum("ac,cms->ams", one_hot(index, columns), own_inc,
                          preferred_element_type=jnp.float32).astype(jnp.bfloat16)

    slot_parts = []
    for g in range(SPAN):
        wanted = request[g * capacity:(g + 1) * capacity]
        slot_parts.append(wanted if g == 1 else passed_along(wanted, "tile", g - 1))
    fetched_parts = []
    for g in range(SPAN):
        picked = pick(slot_parts[g])
        fetched_parts.append(picked if g == 1 else passed_along(picked, "tile", 1 - g))
    packed = adjoints(place, foot_counts, fetched_parts, jac_c, jac_o, innov_c, innov_o, r_blocks)
    recv_parts = []
    for g in range(SPAN):
        piece = packed[g]
        if g == 1:
            recv_parts.append(piece)
        else:
            recv_parts.append(passed_along(piece, "tile", g - 1))
    got_slots = jnp.concatenate(slot_parts, axis=0)
    mine = jnp.einsum("ac,amd->cmd", one_hot(got_slots, columns), jnp.concatenate(recv_parts, axis=0),
                      preferred_element_type=jnp.float32).astype(jnp.bfloat16)
    other = swapped(mine)
    return jnp.where(first, jnp.concatenate([mine, other], axis=1),
                     jnp.concatenate([other, mine], axis=1))


def solution(mesh):
    in_specs = (
        P("tile", "chan", None),
        P("chan", None),
        P("tile", "chan"),
        P("tile", None, None),
        P("tile", None),
        P("tile"),
        P("tile"),
    )
    out_specs = P("tile", None, None)
    return jax.shard_map(
        on_device, mesh=mesh, in_specs=in_specs, out_specs=out_specs, check_vma=False
    )
```

```python
import jax
import jax.numpy as jnp
from jax import lax
from jax.experimental import pallas as pl
from jax.experimental.pallas import tpu as pltpu
from jax.sharding import PartitionSpec as P

SPAN = 4
CAP = 3

NT = (((1,), (1,)), ((), ()))


def passed_along(value, axis, by):
    count = lax.axis_size(axis)
    return lax.ppermute(value, axis, [(i, (i + by) % count) for i in range(count)])


def swapped(value):
    return lax.ppermute(value, "chan", [(0, 1), (1, 0)])


def one_hot(index, size):
    return (index[:, None] == jnp.arange(size, dtype=jnp.int32)[None, :]).astype(jnp.bfloat16)


def adjoint_kernel(place_ref, count_ref, s0_ref, s1_ref, s2_ref, s3_ref, jc_ref, jo_ref, ic_ref, io_ref,
                   rcc_ref, rco_ref, roc_ref, roo_ref, o0_ref, o1_ref, o2_ref, o3_ref,
                   jc_s, jo_s, dc_s, do_s):
    parts = (s0_ref, s1_ref, s2_ref, s3_ref)
    outs = (o0_ref, o1_ref, o2_ref, o3_ref)
    foot = jc_s.shape[0]
    rows = s0_ref.shape[1]
    f = pl.program_id(0)
    group = place_ref[f] // CAP
    rank = place_ref[f] % CAP
    s = parts[3][rank]
    for g in (2, 1, 0):
        s = jnp.where(group == g, parts[g][rank], s)
    for h in range(foot):
        @pl.when(f == h)
        def _():
            jc_s[h] = jc_ref[:, h, :]

    jc = jc_s[f]
    jo = jo_ref[0]
    jo_s[f] = jo
    ev_c = lax.dot_general(s, jc, NT, preferred_element_type=jnp.float32)
    ev_o = lax.dot_general(s, jo, NT, preferred_element_type=jnp.float32)
    at = pl.multiple_of(f * rows, rows)
    dc_s[pl.ds(at, rows), :] = (ev_c - ic_ref[pl.ds(f, 1), :]).astype(jnp.bfloat16)
    do_s[pl.ds(at, rows), :] = (ev_o - io_ref[pl.ds(f, 1), :]).astype(jnp.bfloat16)

    @pl.when(f == foot - 1)
    def _():
        dep_c = dc_s[...]
        dep_o = do_s[...]
        w_c = (jnp.dot(dep_c, rcc_ref[...], preferred_element_type=jnp.float32)
               + jnp.dot(dep_o, roc_ref[...], preferred_element_type=jnp.float32)).astype(jnp.bfloat16)
        w_o = (jnp.dot(dep_c, rco_ref[...], preferred_element_type=jnp.float32)
               + jnp.dot(dep_o, roo_ref[...], preferred_element_type=jnp.float32)).astype(jnp.bfloat16)
        for o_ref in outs:
            o_ref[...] = jnp.zeros(o_ref.shape, o_ref.dtype)
        for h in range(foot):
            adj = (jnp.dot(w_c[h * rows:(h + 1) * rows], jc_s[h], preferred_element_type=jnp.float32)
                   + jnp.dot(w_o[h * rows:(h + 1) * rows], jo_s[h], preferred_element_type=jnp.float32))
            adj = jnp.where(h < count_ref[0], adj, 0.0).astype(jnp.bfloat16)
            grp = place_ref[h] // CAP
            rnk = place_ref[h] % CAP
            for g in range(SPAN):
                @pl.when(grp == g)
                def _():
                    outs[g][rnk] = adj


def adjoints(place, count, fetched, jac_c, jac_o, innov_c, innov_o, r_blocks):
    half_ch, foot, state = jac_c.shape
    half_m = fetched[0].shape[1]
    whole3 = lambda f, p, n: (0, 0, 0)
    whole2 = lambda f, p, n: (0, 0)
    part = pl.BlockSpec(fetched[0].shape, whole3)
    jblock = pl.BlockSpec((1, half_ch, state), lambda f, p, n: (f, 0, 0))
    grid_spec = pltpu.PrefetchScalarGridSpec(
        num_scalar_prefetch=2,
        grid=(foot,),
        in_specs=[part] * SPAN + [pl.BlockSpec((half_ch, foot, state), whole3), jblock,
                                  pl.BlockSpec((foot, half_ch), whole2),
                                  pl.BlockSpec((foot, half_ch), whole2)]
                 + [pl.BlockSpec((half_ch, half_ch), whole2)] * 4,
        out_specs=[pl.BlockSpec((CAP, half_m, state), whole3)] * SPAN,
        scratch_shapes=[pltpu.VMEM((foot, half_ch, state), jnp.bfloat16),
                        pltpu.VMEM((foot, half_ch, state), jnp.bfloat16),
                        pltpu.VMEM((foot * half_m, half_ch), jnp.bfloat16),
                        pltpu.VMEM((foot * half_m, half_ch), jnp.bfloat16)],
    )
    return pl.pallas_call(
        adjoint_kernel,
        grid_spec=grid_spec,
        out_shape=[jax.ShapeDtypeStruct((CAP, half_m, state), jnp.bfloat16)] * SPAN,
    )(place, count, *fetched, jac_c, jac_o, innov_c, innov_o, *r_blocks)


def on_device(jacobian, r_inverse, innovation, increments, owner_offset, column_slot, foot_counts):
    foot = jacobian.shape[0]
    half_ch = jacobian.shape[1]
    columns = increments.shape[0]
    members = increments.shape[1]
    cores = lax.axis_size("chan")
    half_m = members // cores
    core = lax.axis_index("chan")
    capacity = CAP
    slots_total = SPAN * capacity

    jac_c = jnp.transpose(jacobian, (1, 0, 2))
    jac_o = swapped(jacobian)
    innov_c = innovation.astype(jnp.float32)
    innov_o = swapped(innovation).astype(jnp.float32)
    r_o = swapped(r_inverse)
    first = core == 0
    rows_lo = jnp.where(first, r_inverse, r_o)
    rows_hi = jnp.where(first, r_o, r_inverse)
    r00, r01 = rows_lo[:, :half_ch], rows_lo[:, half_ch:]
    r10, r11 = rows_hi[:, :half_ch], rows_hi[:, half_ch:]
    r_blocks = (
        jnp.where(first, r00, r11),
        jnp.where(first, r01, r10),
        jnp.where(first, r10, r01),
        jnp.where(first, r11, r00),
    )

    offset = owner_offset[:, 0]
    order = jnp.arange(foot, dtype=jnp.int32)
    earlier = (offset[:, None] == offset[None, :]) & (order[None, :] < order[:, None])
    rank = jnp.sum(earlier.astype(jnp.int32), axis=1)
    place = offset * capacity + rank
    hit = place[None, :] == jnp.arange(slots_total, dtype=jnp.int32)[:, None]
    request = jnp.sum(jnp.where(hit, column_slot[None, :], 0), axis=1)

    own_inc = lax.dynamic_slice_in_dim(increments, core * half_m, half_m, axis=1)

    def pick(index):
        return jnp.einsum("ac,cms->ams", one_hot(index, columns), own_inc,
                          preferred_element_type=jnp.float32).astype(jnp.bfloat16)

    slot_parts = []
    for g in range(SPAN):
        wanted = request[g * capacity:(g + 1) * capacity]
        slot_parts.append(wanted if g == 1 else passed_along(wanted, "tile", g - 1))
    fetched_parts = []
    for g in range(SPAN):
        picked = pick(slot_parts[g])
        fetched_parts.append(picked if g == 1 else passed_along(picked, "tile", 1 - g))
    packed = adjoints(place, foot_counts, fetched_parts, jac_c, jac_o, innov_c, innov_o, r_blocks)
    recv_parts = []
    for g in range(SPAN):
        piece = packed[g]
        if g == 1:
            recv_parts.append(piece)
        else:
            recv_parts.append(passed_along(piece, "tile", g - 1))
    got_slots = jnp.concatenate(slot_parts, axis=0)
    mine = jnp.einsum("ac,amd->cmd", one_hot(got_slots, columns), jnp.concatenate(recv_parts, axis=0),
                      preferred_element_type=jnp.float32).astype(jnp.bfloat16)
    other = swapped(mine)
    return jnp.where(first, jnp.concatenate([mine, other], axis=1),
                     jnp.concatenate([other, mine], axis=1))


def solution(mesh):
    in_specs = (
        P("tile", "chan", None),
        P("chan", None),
        P("tile", "chan"),
        P("tile", None, None),
        P("tile", None),
        P("tile"),
        P("tile"),
    )
    out_specs = P("tile", None, None)
    return jax.shard_map(
        on_device, mesh=mesh, in_specs=in_specs, out_specs=out_specs, check_vma=False
    )
```

```python
import jax
import jax.numpy as jnp
from jax import lax
from jax.experimental import pallas as pl
from jax.experimental.pallas import tpu as pltpu
from jax.sharding import PartitionSpec as P
from jax.experimental.layout import Layout, with_layout_constraint

SPAN = 4
CAP = 3

NT = (((1,), (1,)), ((), ()))


def passed_along(value, axis, by):
    count = lax.axis_size(axis)
    return lax.ppermute(value, axis, [(i, (i + by) % count) for i in range(count)])


def swapped(value):
    return lax.ppermute(value, "chan", [(0, 1), (1, 0)])


def one_hot(index, size):
    return (index[:, None] == jnp.arange(size, dtype=jnp.int32)[None, :]).astype(jnp.bfloat16)


def adjoint_kernel(place_ref, count_ref, s0_ref, s1_ref, s2_ref, s3_ref, jc_ref, jo_ref, ic_ref, io_ref,
                   rcc_ref, rco_ref, roc_ref, roo_ref, o0_ref, o1_ref, o2_ref, o3_ref,
                   jc_s, jo_s, dc_s, do_s):
    parts = (s0_ref, s1_ref, s2_ref, s3_ref)
    outs = (o0_ref, o1_ref, o2_ref, o3_ref)
    foot = jc_s.shape[0]
    rows = s0_ref.shape[1]
    f = pl.program_id(0)
    group = place_ref[f] // CAP
    rank = place_ref[f] % CAP
    s = parts[3][rank]
    for g in (2, 1, 0):
        s = jnp.where(group == g, parts[g][rank], s)
    for h in range(foot):
        @pl.when(f == h)
        def _():
            jc_s[h] = jc_ref[:, h, :]

    jc = jc_s[f]
    jo = jo_ref[0]
    jo_s[f] = jo
    ev_c = lax.dot_general(s, jc, NT, preferred_element_type=jnp.float32)
    ev_o = lax.dot_general(s, jo, NT, preferred_element_type=jnp.float32)
    at = pl.multiple_of(f * rows, rows)
    dc_s[pl.ds(at, rows), :] = (ev_c - ic_ref[pl.ds(f, 1), :]).astype(jnp.bfloat16)
    do_s[pl.ds(at, rows), :] = (ev_o - io_ref[pl.ds(f, 1), :]).astype(jnp.bfloat16)

    @pl.when(f == foot - 1)
    def _():
        dep_c = dc_s[...]
        dep_o = do_s[...]
        w_c = (jnp.dot(dep_c, rcc_ref[...], preferred_element_type=jnp.float32)
               + jnp.dot(dep_o, roc_ref[...], preferred_element_type=jnp.float32)).astype(jnp.bfloat16)
        w_o = (jnp.dot(dep_c, rco_ref[...], preferred_element_type=jnp.float32)
               + jnp.dot(dep_o, roo_ref[...], preferred_element_type=jnp.float32)).astype(jnp.bfloat16)
        for o_ref in outs:
            o_ref[...] = jnp.zeros(o_ref.shape, o_ref.dtype)
        for h in range(foot):
            adj = (jnp.dot(w_c[h * rows:(h + 1) * rows], jc_s[h], preferred_element_type=jnp.float32)
                   + jnp.dot(w_o[h * rows:(h + 1) * rows], jo_s[h], preferred_element_type=jnp.float32))
            adj = jnp.where(h < count_ref[0], adj, 0.0).astype(jnp.bfloat16)
            grp = place_ref[h] // CAP
            rnk = place_ref[h] % CAP
            for g in range(SPAN):
                @pl.when(grp == g)
                def _():
                    outs[g][rnk] = adj


def adjoints(place, count, fetched, jac_c, jac_o, innov_c, innov_o, r_blocks):
    half_ch, foot, state = jac_c.shape
    half_m = fetched[0].shape[1]
    whole3 = lambda f, p, n: (0, 0, 0)
    whole2 = lambda f, p, n: (0, 0)
    part = pl.BlockSpec(fetched[0].shape, whole3)
    jblock = pl.BlockSpec((1, half_ch, state), lambda f, p, n: (f, 0, 0))
    grid_spec = pltpu.PrefetchScalarGridSpec(
        num_scalar_prefetch=2,
        grid=(foot,),
        in_specs=[part] * SPAN + [pl.BlockSpec((half_ch, foot, state), whole3), jblock,
                                  pl.BlockSpec((foot, half_ch), whole2),
                                  pl.BlockSpec((foot, half_ch), whole2)]
                 + [pl.BlockSpec((half_ch, half_ch), whole2)] * 4,
        out_specs=[pl.BlockSpec((CAP, half_m, state), whole3)] * SPAN,
        scratch_shapes=[pltpu.VMEM((foot, half_ch, state), jnp.bfloat16),
                        pltpu.VMEM((foot, half_ch, state), jnp.bfloat16),
                        pltpu.VMEM((foot * half_m, half_ch), jnp.bfloat16),
                        pltpu.VMEM((foot * half_m, half_ch), jnp.bfloat16)],
    )
    return pl.pallas_call(
        adjoint_kernel,
        grid_spec=grid_spec,
        out_shape=[jax.ShapeDtypeStruct((CAP, half_m, state), jnp.bfloat16)] * SPAN,
    )(place, count, *fetched, jac_c, jac_o, innov_c, innov_o, *r_blocks)


def on_device(jacobian, r_inverse, innovation, increments, owner_offset, column_slot, foot_counts):
    foot = jacobian.shape[0]
    half_ch = jacobian.shape[1]
    columns = increments.shape[0]
    members = increments.shape[1]
    cores = lax.axis_size("chan")
    half_m = members // cores
    core = lax.axis_index("chan")
    capacity = CAP
    slots_total = SPAN * capacity

    jac_c = jnp.transpose(jacobian, (1, 0, 2))
    jac_o = swapped(jacobian)
    innov_c = innovation.astype(jnp.float32)
    innov_o = swapped(innovation).astype(jnp.float32)
    r_o = swapped(r_inverse)
    first = core == 0
    rows_lo = jnp.where(first, r_inverse, r_o)
    rows_hi = jnp.where(first, r_o, r_inverse)
    r00, r01 = rows_lo[:, :half_ch], rows_lo[:, half_ch:]
    r10, r11 = rows_hi[:, :half_ch], rows_hi[:, half_ch:]
    r_blocks = (
        jnp.where(first, r00, r11),
        jnp.where(first, r01, r10),
        jnp.where(first, r10, r01),
        jnp.where(first, r11, r00),
    )

    offset = owner_offset[:, 0]
    order = jnp.arange(foot, dtype=jnp.int32)
    earlier = (offset[:, None] == offset[None, :]) & (order[None, :] < order[:, None])
    rank = jnp.sum(earlier.astype(jnp.int32), axis=1)
    place = offset * capacity + rank
    hit = place[None, :] == jnp.arange(slots_total, dtype=jnp.int32)[:, None]
    request = jnp.sum(jnp.where(hit, column_slot[None, :], 0), axis=1)

    own_inc = lax.dynamic_slice_in_dim(increments, core * half_m, half_m, axis=1)

    def pick(index):
        return jnp.einsum("ac,cms->ams", one_hot(index, columns), own_inc,
                          preferred_element_type=jnp.float32).astype(jnp.bfloat16)

    slot_parts = []
    for g in range(SPAN):
        wanted = request[g * capacity:(g + 1) * capacity]
        slot_parts.append(wanted if g == 1 else passed_along(wanted, "tile", g - 1))
    fetched_parts = []
    for g in range(SPAN):
        picked = pick(slot_parts[g])
        fetched_parts.append(picked if g == 1 else passed_along(picked, "tile", 1 - g))
    packed = adjoints(place, foot_counts, fetched_parts, jac_c, jac_o, innov_c, innov_o, r_blocks)
    recv_parts = []
    for g in range(SPAN):
        piece = packed[g]
        if g == 1:
            recv_parts.append(piece)
        else:
            recv_parts.append(passed_along(piece, "tile", g - 1))
    got_slots = jnp.concatenate(slot_parts, axis=0)
    mine = jnp.einsum("ac,amd->cmd", one_hot(got_slots, columns), jnp.concatenate(recv_parts, axis=0),
                      preferred_element_type=jnp.float32).astype(jnp.bfloat16)
    other = swapped(mine)
    out_order = Layout((2, 0, 1))
    mine = with_layout_constraint(mine, out_order)
    other = with_layout_constraint(other, out_order)
    return jnp.where(first, jnp.concatenate([mine, other], axis=1),
                     jnp.concatenate([other, mine], axis=1))


def solution(mesh):
    in_specs = (
        P("tile", "chan", None),
        P("chan", None),
        P("tile", "chan"),
        P("tile", None, None),
        P("tile", None),
        P("tile"),
        P("tile"),
    )
    out_specs = P("tile", None, None)
    return jax.shard_map(
        on_device, mesh=mesh, in_specs=in_specs, out_specs=out_specs, check_vma=False
    )
```

```python
import jax
import jax.numpy as jnp
from jax import lax
from jax.experimental import pallas as pl
from jax.experimental.pallas import tpu as pltpu
from jax.sharding import PartitionSpec as P

SPAN = 4
CAP = 3

NT = (((1,), (1,)), ((), ()))


def passed_along(value, axis, by):
    count = lax.axis_size(axis)
    return lax.ppermute(value, axis, [(i, (i + by) % count) for i in range(count)])


def swapped(value):
    return lax.ppermute(value, "chan", [(0, 1), (1, 0)])


def one_hot(index, size):
    return (index[:, None] == jnp.arange(size, dtype=jnp.int32)[None, :]).astype(jnp.bfloat16)


def adjoint_kernel(place_ref, count_ref, s0_ref, s1_ref, s2_ref, s3_ref, jc_ref, jo_ref, ic_ref, io_ref,
                   rcc_ref, rco_ref, roc_ref, roo_ref, o0_ref, o1_ref, o2_ref, o3_ref,
                   jc_s, jo_s, dc_s, do_s):
    parts = (s0_ref, s1_ref, s2_ref, s3_ref)
    outs = (o0_ref, o1_ref, o2_ref, o3_ref)
    foot = jc_s.shape[0]
    rows = s0_ref.shape[1]
    f = pl.program_id(0)
    group = place_ref[f] // CAP
    rank = place_ref[f] % CAP
    s = parts[3][rank]
    for g in (2, 1, 0):
        s = jnp.where(group == g, parts[g][rank], s)
    live = f < count_ref[0]
    at = pl.multiple_of(f * rows, rows)

    @pl.when(live)
    def _():
        for h in range(foot):
            @pl.when(f == h)
            def _():
                jc_s[h] = jc_ref[:, h, :]

        jc = jc_s[f]
        jo = jo_ref[0]
        jo_s[f] = jo
        ev_c = lax.dot_general(s, jc, NT, preferred_element_type=jnp.float32)
        ev_o = lax.dot_general(s, jo, NT, preferred_element_type=jnp.float32)
        dc_s[pl.ds(at, rows), :] = (ev_c - ic_ref[pl.ds(f, 1), :]).astype(jnp.bfloat16)
        do_s[pl.ds(at, rows), :] = (ev_o - io_ref[pl.ds(f, 1), :]).astype(jnp.bfloat16)

    @pl.when(jnp.logical_not(live))
    def _():
        dc_s[pl.ds(at, rows), :] = jnp.zeros((rows, dc_s.shape[1]), dc_s.dtype)
        do_s[pl.ds(at, rows), :] = jnp.zeros((rows, do_s.shape[1]), do_s.dtype)

    @pl.when(f == foot - 1)
    def _():
        dep_c = dc_s[...]
        dep_o = do_s[...]
        w_c = (jnp.dot(dep_c, rcc_ref[...], preferred_element_type=jnp.float32)
               + jnp.dot(dep_o, roc_ref[...], preferred_element_type=jnp.float32)).astype(jnp.bfloat16)
        w_o = (jnp.dot(dep_c, rco_ref[...], preferred_element_type=jnp.float32)
               + jnp.dot(dep_o, roo_ref[...], preferred_element_type=jnp.float32)).astype(jnp.bfloat16)
        for o_ref in outs:
            o_ref[...] = jnp.zeros(o_ref.shape, o_ref.dtype)
        for h in range(foot):
            @pl.when(h < count_ref[0])
            def _():
                adj = (jnp.dot(w_c[h * rows:(h + 1) * rows], jc_s[h], preferred_element_type=jnp.float32)
                       + jnp.dot(w_o[h * rows:(h + 1) * rows], jo_s[h], preferred_element_type=jnp.float32))
                adj = adj.astype(jnp.bfloat16)
                grp = place_ref[h] // CAP
                rnk = place_ref[h] % CAP
                for g in range(SPAN):
                    @pl.when(grp == g)
                    def _():
                        outs[g][rnk] = adj


def adjoints(place, count, fetched, jac_c, jac_o, innov_c, innov_o, r_blocks):
    half_ch, foot, state = jac_c.shape
    half_m = fetched[0].shape[1]
    whole3 = lambda f, p, n: (0, 0, 0)
    whole2 = lambda f, p, n: (0, 0)
    part = pl.BlockSpec(fetched[0].shape, whole3)
    jblock = pl.BlockSpec((1, half_ch, state), lambda f, p, n: (f, 0, 0))
    grid_spec = pltpu.PrefetchScalarGridSpec(
        num_scalar_prefetch=2,
        grid=(foot,),
        in_specs=[part] * SPAN + [pl.BlockSpec((half_ch, foot, state), whole3), jblock,
                                  pl.BlockSpec((foot, half_ch), whole2),
                                  pl.BlockSpec((foot, half_ch), whole2)]
                 + [pl.BlockSpec((half_ch, half_ch), whole2)] * 4,
        out_specs=[pl.BlockSpec((CAP, half_m, state), whole3)] * SPAN,
        scratch_shapes=[pltpu.VMEM((foot, half_ch, state), jnp.bfloat16),
                        pltpu.VMEM((foot, half_ch, state), jnp.bfloat16),
                        pltpu.VMEM((foot * half_m, half_ch), jnp.bfloat16),
                        pltpu.VMEM((foot * half_m, half_ch), jnp.bfloat16)],
    )
    return pl.pallas_call(
        adjoint_kernel,
        grid_spec=grid_spec,
        out_shape=[jax.ShapeDtypeStruct((CAP, half_m, state), jnp.bfloat16)] * SPAN,
    )(place, count, *fetched, jac_c, jac_o, innov_c, innov_o, *r_blocks)


def on_device(jacobian, r_inverse, innovation, increments, owner_offset, column_slot, foot_counts):
    foot = jacobian.shape[0]
    half_ch = jacobian.shape[1]
    columns = increments.shape[0]
    members = increments.shape[1]
    cores = lax.axis_size("chan")
    half_m = members // cores
    core = lax.axis_index("chan")
    capacity = CAP
    slots_total = SPAN * capacity

    jac_c = jnp.transpose(jacobian, (1, 0, 2))
    jac_o = swapped(jacobian)
    innov_c = innovation.astype(jnp.float32)
    innov_o = swapped(innovation).astype(jnp.float32)
    r_o = swapped(r_inverse)
    first = core == 0
    rows_lo = jnp.where(first, r_inverse, r_o)
    rows_hi = jnp.where(first, r_o, r_inverse)
    r00, r01 = rows_lo[:, :half_ch], rows_lo[:, half_ch:]
    r10, r11 = rows_hi[:, :half_ch], rows_hi[:, half_ch:]
    r_blocks = (
        jnp.where(first, r00, r11),
        jnp.where(first, r01, r10),
        jnp.where(first, r10, r01),
        jnp.where(first, r11, r00),
    )

    offset = owner_offset[:, 0]
    order = jnp.arange(foot, dtype=jnp.int32)
    earlier = (offset[:, None] == offset[None, :]) & (order[None, :] < order[:, None])
    rank = jnp.sum(earlier.astype(jnp.int32), axis=1)
    place = offset * capacity + rank
    hit = place[None, :] == jnp.arange(slots_total, dtype=jnp.int32)[:, None]
    request = jnp.sum(jnp.where(hit, column_slot[None, :], 0), axis=1)

    own_inc = lax.dynamic_slice_in_dim(increments, core * half_m, half_m, axis=1)

    def pick(index):
        return jnp.einsum("ac,cms->ams", one_hot(index, columns), own_inc,
                          preferred_element_type=jnp.float32).astype(jnp.bfloat16)

    slot_parts = []
    for g in range(SPAN):
        wanted = request[g * capacity:(g + 1) * capacity]
        slot_parts.append(wanted if g == 1 else passed_along(wanted, "tile", g - 1))
    fetched_parts = []
    for g in range(SPAN):
        picked = pick(slot_parts[g])
        fetched_parts.append(picked if g == 1 else passed_along(picked, "tile", 1 - g))
    packed = adjoints(place, foot_counts, fetched_parts, jac_c, jac_o, innov_c, innov_o, r_blocks)
    recv_parts = []
    for g in range(SPAN):
        piece = packed[g]
        if g == 1:
            recv_parts.append(piece)
        else:
            recv_parts.append(passed_along(piece, "tile", g - 1))
    got_slots = jnp.concatenate(slot_parts, axis=0)
    mine = jnp.einsum("ac,amd->cmd", one_hot(got_slots, columns), jnp.concatenate(recv_parts, axis=0),
                      preferred_element_type=jnp.float32).astype(jnp.bfloat16)
    other = swapped(mine)
    return jnp.where(first, jnp.concatenate([mine, other], axis=1),
                     jnp.concatenate([other, mine], axis=1))


def solution(mesh):
    in_specs = (
        P("tile", "chan", None),
        P("chan", None),
        P("tile", "chan"),
        P("tile", None, None),
        P("tile", None),
        P("tile"),
        P("tile"),
    )
    out_specs = P("tile", None, None)
    return jax.shard_map(
        on_device, mesh=mesh, in_specs=in_specs, out_specs=out_specs, check_vma=False
    )
```

```python
import jax
import jax.numpy as jnp
from jax import lax
from jax.experimental import pallas as pl
from jax.experimental.pallas import tpu as pltpu
from jax.sharding import PartitionSpec as P

SPAN = 4
CAP = 3

NT = (((1,), (1,)), ((), ()))


def passed_along(value, axis, by):
    count = lax.axis_size(axis)
    return lax.ppermute(value, axis, [(i, (i + by) % count) for i in range(count)])


def swapped(value):
    return lax.ppermute(value, "chan", [(0, 1), (1, 0)])


def one_hot(index, size):
    return (index[:, None] == jnp.arange(size, dtype=jnp.int32)[None, :]).astype(jnp.bfloat16)


def adjoint_kernel(place_ref, count_ref, s0_ref, s1_ref, s2_ref, s3_ref, jc_ref, jo_ref, ic_ref, io_ref,
                   rcc_ref, rco_ref, roc_ref, roo_ref, o0_ref, o1_ref, o2_ref, o3_ref,
                   jc_s, jo_s, dc_s, do_s):
    parts = (s0_ref, s1_ref, s2_ref, s3_ref)
    outs = (o0_ref, o1_ref, o2_ref, o3_ref)
    foot = jc_s.shape[0]
    rows = s0_ref.shape[1]
    f = pl.program_id(0)
    group = place_ref[f] // CAP
    rank = place_ref[f] % CAP
    s = parts[3][rank]
    for g in (2, 1, 0):
        s = jnp.where(group == g, parts[g][rank], s)
    for h in range(foot):
        @pl.when(f == h)
        def _():
            jc_s[h] = jc_ref[:, h, :]

    jc = jc_s[f]
    jo = jo_ref[0]
    jo_s[f] = jo
    ev_c = lax.dot_general(s, jc, NT, preferred_element_type=jnp.float32)
    ev_o = lax.dot_general(s, jo, NT, preferred_element_type=jnp.float32)
    at = pl.multiple_of(f * rows, rows)
    dc_s[pl.ds(at, rows), :] = (ev_c - ic_ref[pl.ds(f, 1), :]).astype(jnp.bfloat16)
    do_s[pl.ds(at, rows), :] = (ev_o - io_ref[pl.ds(f, 1), :]).astype(jnp.bfloat16)

    @pl.when(f == foot - 1)
    def _():
        dep_c = dc_s[...]
        dep_o = do_s[...]
        w_c = (jnp.dot(dep_c, rcc_ref[...], preferred_element_type=jnp.float32)
               + jnp.dot(dep_o, roc_ref[...], preferred_element_type=jnp.float32)).astype(jnp.bfloat16)
        w_o = (jnp.dot(dep_c, rco_ref[...], preferred_element_type=jnp.float32)
               + jnp.dot(dep_o, roo_ref[...], preferred_element_type=jnp.float32)).astype(jnp.bfloat16)
        for o_ref in outs:
            o_ref[...] = jnp.zeros(o_ref.shape, o_ref.dtype)
        for h in range(foot):
            adj = (jnp.dot(w_c[h * rows:(h + 1) * rows], jc_s[h], preferred_element_type=jnp.float32)
                   + jnp.dot(w_o[h * rows:(h + 1) * rows], jo_s[h], preferred_element_type=jnp.float32))
            adj = jnp.where(h < count_ref[0], adj, 0.0).astype(jnp.bfloat16)
            grp = place_ref[h] // CAP
            rnk = place_ref[h] % CAP
            for g in range(SPAN):
                @pl.when(grp == g)
                def _():
                    outs[g][rnk] = adj


def adjoints(place, count, fetched, jac_c, jac_o, innov_c, innov_o, r_blocks):
    half_ch, foot, state = jac_c.shape
    half_m = fetched[0].shape[1]
    whole3 = lambda f, p, n: (0, 0, 0)
    whole2 = lambda f, p, n: (0, 0)
    part = pl.BlockSpec(fetched[0].shape, whole3)
    jblock = pl.BlockSpec((1, half_ch, state), lambda f, p, n: (f, 0, 0))
    grid_spec = pltpu.PrefetchScalarGridSpec(
        num_scalar_prefetch=2,
        grid=(foot,),
        in_specs=[part] * SPAN + [pl.BlockSpec((half_ch, foot, state), whole3), jblock,
                                  pl.BlockSpec((foot, half_ch), whole2),
                                  pl.BlockSpec((foot, half_ch), whole2)]
                 + [pl.BlockSpec((half_ch, half_ch), whole2)] * 4,
        out_specs=[pl.BlockSpec((CAP, half_m, state), whole3)] * SPAN,
        scratch_shapes=[pltpu.VMEM((foot, half_ch, state), jnp.bfloat16),
                        pltpu.VMEM((foot, half_ch, state), jnp.bfloat16),
                        pltpu.VMEM((foot * half_m, half_ch), jnp.bfloat16),
                        pltpu.VMEM((foot * half_m, half_ch), jnp.bfloat16)],
    )
    return pl.pallas_call(
        adjoint_kernel,
        grid_spec=grid_spec,
        out_shape=[jax.ShapeDtypeStruct((CAP, half_m, state), jnp.bfloat16)] * SPAN,
    )(place, count, *fetched, jac_c, jac_o, innov_c, innov_o, *r_blocks)


def on_device(jacobian, r_inverse, innovation, increments, owner_offset, column_slot, foot_counts):
    foot = jacobian.shape[0]
    half_ch = jacobian.shape[1]
    columns = increments.shape[0]
    members = increments.shape[1]
    cores = lax.axis_size("chan")
    half_m = members // cores
    core = lax.axis_index("chan")
    capacity = CAP
    slots_total = SPAN * capacity

    jac_c = jnp.transpose(jacobian, (1, 0, 2))
    jac_o = swapped(jacobian)
    innov_c = innovation.astype(jnp.float32)
    innov_o = swapped(innovation).astype(jnp.float32)
    r_o = swapped(r_inverse)
    first = core == 0
    rows_lo = jnp.where(first, r_inverse, r_o)
    rows_hi = jnp.where(first, r_o, r_inverse)
    r00, r01 = rows_lo[:, :half_ch], rows_lo[:, half_ch:]
    r10, r11 = rows_hi[:, :half_ch], rows_hi[:, half_ch:]
    r_blocks = (
        jnp.where(first, r00, r11),
        jnp.where(first, r01, r10),
        jnp.where(first, r10, r01),
        jnp.where(first, r11, r00),
    )

    offset = owner_offset[:, 0]
    order = jnp.arange(foot, dtype=jnp.int32)
    earlier = (offset[:, None] == offset[None, :]) & (order[None, :] < order[:, None])
    rank = jnp.sum(earlier.astype(jnp.int32), axis=1)
    place = offset * capacity + rank
    hit = place[None, :] == jnp.arange(slots_total, dtype=jnp.int32)[:, None]
    request = jnp.sum(jnp.where(hit, column_slot[None, :], 0), axis=1)

    own_inc = lax.dynamic_slice_in_dim(increments, core * half_m, half_m, axis=1)

    def pick(index):
        return jnp.einsum("ac,cms->ams", one_hot(index, columns), own_inc,
                          preferred_element_type=jnp.float32).astype(jnp.bfloat16)

    slot_parts = []
    for g in range(SPAN):
        wanted = request[g * capacity:(g + 1) * capacity]
        slot_parts.append(wanted if g == 1 else passed_along(wanted, "tile", g - 1))
    fetched_parts = []
    for g in range(SPAN):
        picked = pick(slot_parts[g])
        fetched_parts.append(picked if g == 1 else passed_along(picked, "tile", 1 - g))
    packed = adjoints(place, foot_counts, fetched_parts, jac_c, jac_o, innov_c, innov_o, r_blocks)
    recv_parts = []
    for g in range(SPAN):
        piece = packed[g]
        if g == 1:
            recv_parts.append(piece)
        else:
            recv_parts.append(passed_along(piece, "tile", g - 1))
    got_slots = jnp.concatenate(slot_parts, axis=0)
    mine = jnp.einsum("ac,amd->cmd", one_hot(got_slots, columns), jnp.concatenate(recv_parts, axis=0),
                      preferred_element_type=jnp.float32).astype(jnp.bfloat16)
    other = swapped(mine)
    full = jnp.zeros((columns, members, mine.shape[2]), mine.dtype)
    full = lax.dynamic_update_slice_in_dim(full, mine, core * half_m, axis=1)
    return lax.dynamic_update_slice_in_dim(full, other, (1 - core) * half_m, axis=1)


def solution(mesh):
    in_specs = (
        P("tile", "chan", None),
        P("chan", None),
        P("tile", "chan"),
        P("tile", None, None),
        P("tile", None),
        P("tile"),
        P("tile"),
    )
    out_specs = P("tile", None, None)
    return jax.shard_map(
        on_device, mesh=mesh, in_specs=in_specs, out_specs=out_specs, check_vma=False
    )
```

```python
import jax
import jax.numpy as jnp
from jax import lax
from jax.experimental import pallas as pl
from jax.experimental.pallas import tpu as pltpu
from jax.sharding import PartitionSpec as P

SPAN = 4
CAP = 3

NT = (((1,), (1,)), ((), ()))


def passed_along(value, axis, by):
    count = lax.axis_size(axis)
    return lax.ppermute(value, axis, [(i, (i + by) % count) for i in range(count)])


def swapped(value):
    return lax.ppermute(value, "chan", [(0, 1), (1, 0)])


def one_hot(index, size):
    return (index[:, None] == jnp.arange(size, dtype=jnp.int32)[None, :]).astype(jnp.bfloat16)


def adjoint_kernel(place_ref, count_ref, s0_ref, s1_ref, s2_ref, s3_ref, jc_ref, jo_ref, ic_ref, io_ref,
                   rcc_ref, rco_ref, roc_ref, roo_ref, o0_ref, o1_ref, o2_ref, o3_ref,
                   jc_s, jo_s, dc_s, do_s):
    parts = (s0_ref, s1_ref, s2_ref, s3_ref)
    outs = (o0_ref, o1_ref, o2_ref, o3_ref)
    foot = jc_s.shape[0]
    rows = s0_ref.shape[1]
    f = pl.program_id(0)
    group = place_ref[f] // CAP
    rank = place_ref[f] % CAP
    s = parts[3][rank]
    for g in (2, 1, 0):
        s = jnp.where(group == g, parts[g][rank], s)
    for h in range(foot):
        @pl.when(f == h)
        def _():
            jc_s[h] = jc_ref[:, h, :]

    jc = jc_s[f]
    jo = jo_ref[0]
    jo_s[f] = jo
    ev_c = lax.dot_general(s, jc, NT, preferred_element_type=jnp.float32)
    ev_o = lax.dot_general(s, jo, NT, preferred_element_type=jnp.float32)
    at = pl.multiple_of(f * rows, rows)
    dc_s[pl.ds(at, rows), :] = (ev_c - ic_ref[pl.ds(f, 1), :]).astype(jnp.bfloat16)
    do_s[pl.ds(at, rows), :] = (ev_o - io_ref[pl.ds(f, 1), :]).astype(jnp.bfloat16)

    @pl.when(f == foot - 1)
    def _():
        dep_c = dc_s[...]
        dep_o = do_s[...]
        w_c = (jnp.dot(dep_c, rcc_ref[...], preferred_element_type=jnp.float32)
               + jnp.dot(dep_o, roc_ref[...], preferred_element_type=jnp.float32)).astype(jnp.bfloat16)
        w_o = (jnp.dot(dep_c, rco_ref[...], preferred_element_type=jnp.float32)
               + jnp.dot(dep_o, roo_ref[...], preferred_element_type=jnp.float32)).astype(jnp.bfloat16)
        for o_ref in outs:
            o_ref[...] = jnp.zeros(o_ref.shape, o_ref.dtype)
        for h in range(foot):
            adj = (jnp.dot(w_c[h * rows:(h + 1) * rows], jc_s[h], preferred_element_type=jnp.float32)
                   + jnp.dot(w_o[h * rows:(h + 1) * rows], jo_s[h], preferred_element_type=jnp.float32))
            adj = jnp.where(h < count_ref[0], adj, 0.0).astype(jnp.bfloat16)
            grp = place_ref[h] // CAP
            rnk = place_ref[h] % CAP
            for g in range(SPAN):
                @pl.when(grp == g)
                def _():
                    outs[g][rnk] = adj


def adjoints(place, count, fetched, jac_c, jac_o, innov_c, innov_o, r_blocks):
    half_ch, foot, state = jac_c.shape
    half_m = fetched[0].shape[1]
    whole3 = lambda f, p, n: (0, 0, 0)
    whole2 = lambda f, p, n: (0, 0)
    part = pl.BlockSpec(fetched[0].shape, whole3)
    jblock = pl.BlockSpec((1, half_ch, state), lambda f, p, n: (f, 0, 0))
    grid_spec = pltpu.PrefetchScalarGridSpec(
        num_scalar_prefetch=2,
        grid=(foot,),
        in_specs=[part] * SPAN + [pl.BlockSpec((half_ch, foot, state), whole3), jblock,
                                  pl.BlockSpec((foot, half_ch), whole2),
                                  pl.BlockSpec((foot, half_ch), whole2)]
                 + [pl.BlockSpec((half_ch, half_ch), whole2)] * 4,
        out_specs=[pl.BlockSpec((CAP, half_m, state), whole3)] * SPAN,
        scratch_shapes=[pltpu.VMEM((foot, half_ch, state), jnp.bfloat16),
                        pltpu.VMEM((foot, half_ch, state), jnp.bfloat16),
                        pltpu.VMEM((foot * half_m, half_ch), jnp.bfloat16),
                        pltpu.VMEM((foot * half_m, half_ch), jnp.bfloat16)],
    )
    return pl.pallas_call(
        adjoint_kernel,
        grid_spec=grid_spec,
        out_shape=[jax.ShapeDtypeStruct((CAP, half_m, state), jnp.bfloat16)] * SPAN,
    )(place, count, *fetched, jac_c, jac_o, innov_c, innov_o, *r_blocks)


def on_device(jacobian, r_inverse, innovation, increments, owner_offset, column_slot, foot_counts):
    foot = jacobian.shape[0]
    half_ch = jacobian.shape[1]
    columns = increments.shape[0]
    members = increments.shape[1]
    cores = lax.axis_size("chan")
    half_m = members // cores
    core = lax.axis_index("chan")
    capacity = CAP
    slots_total = SPAN * capacity

    jac_c = jnp.transpose(jacobian, (1, 0, 2))
    jac_o = swapped(jacobian)
    innov_c = innovation.astype(jnp.float32)
    innov_o = swapped(innovation).astype(jnp.float32)
    r_o = swapped(r_inverse)
    first = core == 0
    rows_lo = jnp.where(first, r_inverse, r_o)
    rows_hi = jnp.where(first, r_o, r_inverse)
    r00, r01 = rows_lo[:, :half_ch], rows_lo[:, half_ch:]
    r10, r11 = rows_hi[:, :half_ch], rows_hi[:, half_ch:]
    r_blocks = (
        jnp.where(first, r00, r11),
        jnp.where(first, r01, r10),
        jnp.where(first, r10, r01),
        jnp.where(first, r11, r00),
    )

    offset = owner_offset[:, 0]
    order = jnp.arange(foot, dtype=jnp.int32)
    earlier = (offset[:, None] == offset[None, :]) & (order[None, :] < order[:, None])
    rank = jnp.sum(earlier.astype(jnp.int32), axis=1)
    place = offset * capacity + rank
    hit = place[None, :] == jnp.arange(slots_total, dtype=jnp.int32)[:, None]
    request = jnp.sum(jnp.where(hit, column_slot[None, :], 0), axis=1)

    own_inc = lax.dynamic_slice_in_dim(increments, core * half_m, half_m, axis=1)

    def pick(index):
        return jnp.einsum("ac,cms->ams", one_hot(index, columns), own_inc,
                          preferred_element_type=jnp.float32).astype(jnp.bfloat16)

    issue = (3, 2, 0, 1)
    slot_parts = [None] * SPAN
    for g in issue:
        wanted = request[g * capacity:(g + 1) * capacity]
        slot_parts[g] = wanted if g == 1 else passed_along(wanted, "tile", g - 1)
    fetched_parts = [None] * SPAN
    for g in issue:
        picked = pick(slot_parts[g])
        fetched_parts[g] = picked if g == 1 else passed_along(picked, "tile", 1 - g)
    packed = adjoints(place, foot_counts, fetched_parts, jac_c, jac_o, innov_c, innov_o, r_blocks)
    recv_parts = []
    for g in range(SPAN):
        piece = packed[g]
        if g == 1:
            recv_parts.append(piece)
        else:
            recv_parts.append(passed_along(piece, "tile", g - 1))
    got_slots = jnp.concatenate(slot_parts, axis=0)
    mine = jnp.einsum("ac,amd->cmd", one_hot(got_slots, columns), jnp.concatenate(recv_parts, axis=0),
                      preferred_element_type=jnp.float32).astype(jnp.bfloat16)
    other = swapped(mine)
    return jnp.where(first, jnp.concatenate([mine, other], axis=1),
                     jnp.concatenate([other, mine], axis=1))


def solution(mesh):
    in_specs = (
        P("tile", "chan", None),
        P("chan", None),
        P("tile", "chan"),
        P("tile", None, None),
        P("tile", None),
        P("tile"),
        P("tile"),
    )
    out_specs = P("tile", None, None)
    return jax.shard_map(
        on_device, mesh=mesh, in_specs=in_specs, out_specs=out_specs, check_vma=False
    )
```

```python
import jax
import jax.numpy as jnp
from jax import lax
from jax.experimental import pallas as pl
from jax.experimental.pallas import tpu as pltpu
from jax.sharding import PartitionSpec as P

SPAN = 4
CAP = 3

NT = (((1,), (1,)), ((), ()))


def passed_along(value, axis, by):
    count = lax.axis_size(axis)
    return lax.ppermute(value, axis, [(i, (i + by) % count) for i in range(count)])


def swapped(value):
    return lax.ppermute(value, "chan", [(0, 1), (1, 0)])


def one_hot(index, size):
    return (index[:, None] == jnp.arange(size, dtype=jnp.int32)[None, :]).astype(jnp.bfloat16)


def adjoint_kernel(place_ref, count_ref, s0_ref, s1_ref, s2_ref, s3_ref, jc_ref, jo_ref, ic_ref, io_ref,
                   rcc_ref, rco_ref, roc_ref, roo_ref, o0_ref, o1_ref, o2_ref, o3_ref,
                   jc_s, jo_s, dc_s, do_s):
    parts = (s0_ref, s1_ref, s2_ref, s3_ref)
    outs = (o0_ref, o1_ref, o2_ref, o3_ref)
    foot = jc_s.shape[0]
    rows = s0_ref.shape[1]
    f = pl.program_id(0)
    group = place_ref[f] // CAP
    rank = place_ref[f] % CAP
    s = parts[3][rank]
    for g in (2, 1, 0):
        s = jnp.where(group == g, parts[g][rank], s)
    for h in range(foot):
        @pl.when(f == h)
        def _():
            jc_s[h] = jc_ref[:, h, :]

    jc = jc_s[f]
    jo = jo_ref[0]
    jo_s[f] = jo
    ev_c = lax.dot_general(s, jc, NT, preferred_element_type=jnp.float32)
    ev_o = lax.dot_general(s, jo, NT, preferred_element_type=jnp.float32)
    at = pl.multiple_of(f * rows, rows)
    which = lax.broadcasted_iota(jnp.int32, ic_ref.shape, 0) == f
    innov_row_c = jnp.sum(jnp.where(which, ic_ref[...].astype(jnp.float32), 0.0), axis=0, keepdims=True)
    innov_row_o = jnp.sum(jnp.where(which, io_ref[...].astype(jnp.float32), 0.0), axis=0, keepdims=True)
    dc_s[pl.ds(at, rows), :] = (ev_c - innov_row_c).astype(jnp.bfloat16)
    do_s[pl.ds(at, rows), :] = (ev_o - innov_row_o).astype(jnp.bfloat16)

    @pl.when(f == foot - 1)
    def _():
        dep_c = dc_s[...]
        dep_o = do_s[...]
        w_c = (jnp.dot(dep_c, rcc_ref[...], preferred_element_type=jnp.float32)
               + jnp.dot(dep_o, roc_ref[...], preferred_element_type=jnp.float32)).astype(jnp.bfloat16)
        w_o = (jnp.dot(dep_c, rco_ref[...], preferred_element_type=jnp.float32)
               + jnp.dot(dep_o, roo_ref[...], preferred_element_type=jnp.float32)).astype(jnp.bfloat16)
        for o_ref in outs:
            o_ref[...] = jnp.zeros(o_ref.shape, o_ref.dtype)
        for h in range(foot):
            adj = (jnp.dot(w_c[h * rows:(h + 1) * rows], jc_s[h], preferred_element_type=jnp.float32)
                   + jnp.dot(w_o[h * rows:(h + 1) * rows], jo_s[h], preferred_element_type=jnp.float32))
            adj = jnp.where(h < count_ref[0], adj, 0.0).astype(jnp.bfloat16)
            grp = place_ref[h] // CAP
            rnk = place_ref[h] % CAP
            for g in range(SPAN):
                @pl.when(grp == g)
                def _():
                    outs[g][rnk] = adj


def adjoints(place, count, fetched, jac_c, jac_o, innov_c, innov_o, r_blocks):
    half_ch, foot, state = jac_c.shape
    half_m = fetched[0].shape[1]
    whole3 = lambda f, p, n: (0, 0, 0)
    whole2 = lambda f, p, n: (0, 0)
    part = pl.BlockSpec(fetched[0].shape, whole3)
    jblock = pl.BlockSpec((1, half_ch, state), lambda f, p, n: (f, 0, 0))
    grid_spec = pltpu.PrefetchScalarGridSpec(
        num_scalar_prefetch=2,
        grid=(foot,),
        in_specs=[part] * SPAN + [pl.BlockSpec((half_ch, foot, state), whole3), jblock,
                                  pl.BlockSpec((foot, half_ch), whole2),
                                  pl.BlockSpec((foot, half_ch), whole2)]
                 + [pl.BlockSpec((half_ch, half_ch), whole2)] * 4,
        out_specs=[pl.BlockSpec((CAP, half_m, state), whole3)] * SPAN,
        scratch_shapes=[pltpu.VMEM((foot, half_ch, state), jnp.bfloat16),
                        pltpu.VMEM((foot, half_ch, state), jnp.bfloat16),
                        pltpu.VMEM((foot * half_m, half_ch), jnp.bfloat16),
                        pltpu.VMEM((foot * half_m, half_ch), jnp.bfloat16)],
    )
    return pl.pallas_call(
        adjoint_kernel,
        grid_spec=grid_spec,
        out_shape=[jax.ShapeDtypeStruct((CAP, half_m, state), jnp.bfloat16)] * SPAN,
    )(place, count, *fetched, jac_c, jac_o, innov_c, innov_o, *r_blocks)


def on_device(jacobian, r_inverse, innovation, increments, owner_offset, column_slot, foot_counts):
    foot = jacobian.shape[0]
    half_ch = jacobian.shape[1]
    columns = increments.shape[0]
    members = increments.shape[1]
    cores = lax.axis_size("chan")
    half_m = members // cores
    core = lax.axis_index("chan")
    capacity = CAP
    slots_total = SPAN * capacity

    jac_c = jnp.transpose(jacobian, (1, 0, 2))
    jac_o = swapped(jacobian)
    innov_c = innovation
    innov_o = swapped(innovation)
    r_o = swapped(r_inverse)
    first = core == 0
    rows_lo = jnp.where(first, r_inverse, r_o)
    rows_hi = jnp.where(first, r_o, r_inverse)
    r00, r01 = rows_lo[:, :half_ch], rows_lo[:, half_ch:]
    r10, r11 = rows_hi[:, :half_ch], rows_hi[:, half_ch:]
    r_blocks = (
        jnp.where(first, r00, r11),
        jnp.where(first, r01, r10),
        jnp.where(first, r10, r01),
        jnp.where(first, r11, r00),
    )

    offset = owner_offset[:, 0]
    order = jnp.arange(foot, dtype=jnp.int32)
    earlier = (offset[:, None] == offset[None, :]) & (order[None, :] < order[:, None])
    rank = jnp.sum(earlier.astype(jnp.int32), axis=1)
    place = offset * capacity + rank
    hit = place[None, :] == jnp.arange(slots_total, dtype=jnp.int32)[:, None]
    request = jnp.sum(jnp.where(hit, column_slot[None, :], 0), axis=1)

    own_inc = lax.dynamic_slice_in_dim(increments, core * half_m, half_m, axis=1)

    def pick(index):
        return jnp.einsum("ac,cms->ams", one_hot(index, columns), own_inc,
                          preferred_element_type=jnp.float32).astype(jnp.bfloat16)

    slot_parts = []
    for g in range(SPAN):
        wanted = request[g * capacity:(g + 1) * capacity]
        slot_parts.append(wanted if g == 1 else passed_along(wanted, "tile", g - 1))
    fetched_parts = []
    for g in range(SPAN):
        picked = pick(slot_parts[g])
        fetched_parts.append(picked if g == 1 else passed_along(picked, "tile", 1 - g))
    packed = adjoints(place, foot_counts, fetched_parts, jac_c, jac_o, innov_c, innov_o, r_blocks)
    recv_parts = []
    for g in range(SPAN):
        piece = packed[g]
        if g == 1:
            recv_parts.append(piece)
        else:
            recv_parts.append(passed_along(piece, "tile", g - 1))
    got_slots = jnp.concatenate(slot_parts, axis=0)
    mine = jnp.einsum("ac,amd->cmd", one_hot(got_slots, columns), jnp.concatenate(recv_parts, axis=0),
                      preferred_element_type=jnp.float32).astype(jnp.bfloat16)
    other = swapped(mine)
    return jnp.where(first, jnp.concatenate([mine, other], axis=1),
                     jnp.concatenate([other, mine], axis=1))


def solution(mesh):
    in_specs = (
        P("tile", "chan", None),
        P("chan", None),
        P("tile", "chan"),
        P("tile", None, None),
        P("tile", None),
        P("tile"),
        P("tile"),
    )
    out_specs = P("tile", None, None)
    return jax.shard_map(
        on_device, mesh=mesh, in_specs=in_specs, out_specs=out_specs, check_vma=False
    )
```
